256 devices in a mesh: blk: 32 (over y, z), tp: 8 (over x, core).
Axes of the slice: x: 4, y: 4, z: 8, core: 2. Of those that a mesh axis runs over, the one named last changes fastest.
Arguments:
- queries: bfloat16 [32768, 1664], P(('blk', 'tp')), may hold values from -120 to 120
- keys: bfloat16 [32768, 1664], P(('blk', 'tp')), may hold values from -6 to 6
- values: bfloat16 [32768, 1664], P(('blk', 'tp')), may hold values from -6 to 6
- segment_ids: int32 [32768], replicated, may hold values from -1 to 31, as said below
- proj_weight: bfloat16 [6656, 3072], P(None, 'tp'), may hold values from -0.078125 to 0.078125
Outputs:
- normed: bfloat16 [8192, 3072], P('blk', 'tp')
- seg_peaks: float32 [32], replicated
The draws below stay inside these ranges and needn't reach their ends.
Inputs may be any that keep to these rules, and one draw needn't show every extreme that they name: `segment_ids`: ids other than -1 never fall along the pack; every image 0 to 31 occurs as one run of tokens that starts at a multiple of 4 and has a multiple of 4 tokens, at most 1024; some image has exactly 1024; -1 marks padding tokens, which may stand between images.
All inputs are finite; a program needn't handle non-finite values.
Results may differ from the reference program's by a relative error of at most 0.0056.
Values may be sent and summed in bfloat16 or wider, within the bound.
No kernel may reach another device: no remote copies, remote signals or barrier semaphores. Data moves between devices by JAX's collectives and lax.ppermute only.
A program may use at most 128 MiB of HBM per device.

```python
import jax
import jax.numpy as jnp
from jax import lax

TOK_DEV = 1024
HEAD = 128
NOUT = 3072
HD = 1664
MERGED = 6656
TOKENS = 32768
MROWS = 8192
SEGS = 32
MOST = 256
N_BLK = 32


def shared_rows(key):
    key_rows = jnp.clip(jax.random.normal(jax.random.fold_in(key, 101), (TOKENS, HD), jnp.float32), -6.0, 6.0)
    query_rows = jnp.clip(jax.random.normal(jax.random.fold_in(key, 202), (TOKENS, HD), jnp.float32), -6.0, 6.0)
    return (query_rows, key_rows)


def draw_queries(key, part):
    return shared_rows(key)[0].astype(jnp.bfloat16)


def draw_keys(key, part):
    return shared_rows(key)[1].astype(jnp.bfloat16)


def draw_segment_ids(key, part):
    first_key, second_key, third_key = jax.random.split(jax.random.fold_in(key, 7), 3)
    least = max(1, MOST // 8)
    quarter = MOST // 4
    image_index = jnp.arange(SEGS, dtype=jnp.int32)
    chosen = jax.random.randint(third_key, (), 1, SEGS, dtype=jnp.int32)
    heads_part = jax.random.randint(first_key, (SEGS,), least, MOST - least + 1, dtype=jnp.int32)
    heads_part = jnp.where(image_index == chosen, quarter, heads_part)
    heads_part = jnp.where(image_index == chosen - 1, jnp.minimum(heads_part, quarter), heads_part)
    heads_before = jnp.concatenate([jnp.zeros((1,), jnp.int32), heads_part[:-1]])
    tail_cap = jnp.minimum(MOST - heads_before, MOST - heads_part)
    tails_part = jax.random.randint(second_key, (SEGS,), least, tail_cap + 1, dtype=jnp.int32)
    tails_part = jnp.where(image_index == chosen, MOST - quarter, tails_part)
    tails_part = jnp.where(image_index == 0, 0, tails_part)
    position = jnp.arange(MROWS, dtype=jnp.int32)
    block = position // MOST
    offset = position % MOST
    next_image = jnp.minimum(block + 1, SEGS - 1)
    head_len = jnp.take(heads_part, block)
    tail_len = jnp.take(tails_part, next_image)
    in_head = offset < head_len
    in_tail = (offset >= MOST - tail_len) & (block + 1 < SEGS)
    merged_ids = jnp.where(in_head, block, jnp.where(in_tail, block + 1, -1))
    return jnp.repeat(merged_ids.astype(jnp.int32), 4)


def levels(rng, shape, cuts, low, largest):
    gain, own = 1.0, jax.random.fold_in(rng, 6)
    for axis_at, parts in cuts:
        heights = jnp.exp(jax.random.uniform(jax.random.fold_in(own, axis_at), (parts,), jnp.float32, low / len(cuts), largest / len(cuts)))
        gain = gain * jnp.repeat(heights, shape[axis_at] // parts).reshape([-1 if axis == axis_at else 1 for axis in range(len(shape))])
    return gain


def gaussian(rng, shape, scale, bound, pieces=(), held_as=jnp.bfloat16):
    loudness = levels(rng, shape, pieces, -0.22, 0.18) if pieces else 1.0
    values = jax.random.normal(rng, shape, jnp.float32) * scale * loudness
    return jnp.minimum(jnp.maximum(values, -bound), bound).astype(held_as)


def setup_inputs(seed: int = 0) -> dict:
    key_list = jax.random.split(jax.random.key(seed), 6)
    return {
        "queries": draw_queries(jax.random.fold_in(key_list[5], 71), 0),
        "keys": draw_keys(jax.random.fold_in(key_list[5], 71), 0),
        "values": gaussian(key_list[2], (TOKENS, HD), 1.0, 6.0, ((0, 256),)),
        "segment_ids": draw_segment_ids(jax.random.fold_in(key_list[5], 71), 0),
        "proj_weight": gaussian(key_list[4], (MERGED, NOUT), MERGED ** -0.5, 0.078125, ((1, 8),)),
    }


masked_score = -1e+30
epsilon = 1e-06

def finish(scores, allowed, value_heads):
    scores = jnp.where(allowed[None], scores, masked_score)
    row_top = lax.optimization_barrier(jnp.max(scores, axis=2, keepdims=True))
    exp_terms = jnp.where(allowed[None], jnp.exp(scores - row_top), 0.0)
    row_total = jnp.maximum(lax.optimization_barrier(jnp.sum(exp_terms, axis=2)), 1.0)
    weights = exp_terms.astype(jnp.bfloat16).astype(jnp.float32)
    mixed_out = jnp.einsum('hrk,khd->rhd', weights, value_heads.astype(jnp.float32))
    return mixed_out / row_total.T[:, :, None]

def reference(queries, keys, values, segment_ids, proj_weight):
    heads_count = queries.shape[1] // HEAD
    zero_rows = jnp.zeros((TOK_DEV, queries.shape[1]), jnp.bfloat16)
    padded_keys = jnp.concatenate([zero_rows, keys, zero_rows], axis=0)
    padded_values = jnp.concatenate([zero_rows, values, zero_rows], axis=0)
    edge_segs = jnp.full((TOK_DEV,), -2, jnp.int32)
    padded_segs = jnp.concatenate([edge_segs, segment_ids, edge_segs], axis=0)

    def one_block(index):
        first_row = (index * TOK_DEV).astype(jnp.int32)
        query_rows = lax.dynamic_slice_in_dim(queries, first_row, TOK_DEV)
        query_segs = lax.dynamic_slice_in_dim(segment_ids, first_row, TOK_DEV)
        key_rows = lax.dynamic_slice_in_dim(padded_keys, first_row, 3 * TOK_DEV)
        value_rows = lax.dynamic_slice_in_dim(padded_values, first_row, 3 * TOK_DEV)
        key_segs = lax.dynamic_slice_in_dim(padded_segs, first_row, 3 * TOK_DEV)
        query_heads = query_rows.reshape(TOK_DEV, heads_count, HEAD).astype(jnp.float32)
        key_heads = key_rows.reshape(3 * TOK_DEV, heads_count, HEAD).astype(jnp.float32)
        value_heads = value_rows.reshape(3 * TOK_DEV, heads_count, HEAD)
        scores = jnp.einsum('rhd,khd->hrk', query_heads, key_heads) * HEAD ** (-0.5)
        allowed = (query_segs[:, None] == key_segs[None, :]) & (query_segs[:, None] >= 0)
        mixed_out = finish(scores, allowed, value_heads)
        return mixed_out.reshape(TOK_DEV, heads_count * HEAD).astype(jnp.bfloat16)
    attended = lax.map(one_block, jnp.arange(N_BLK, dtype=jnp.int32))
    attended = attended.reshape(TOKENS, queries.shape[1])
    merged = attended.reshape(MROWS, 4 * queries.shape[1])
    projected = jnp.dot(merged, proj_weight, preferred_element_type=jnp.float32)
    row_segs = segment_ids[::4]
    member = row_segs[:, None] == jnp.arange(SEGS, dtype=jnp.int32)[None, :]
    squares = lax.optimization_barrier(jnp.sum(projected * projected, axis=1))
    seg_sums = lax.optimization_barrier(jnp.sum(jnp.where(member, squares[:, None], 0.0), axis=0))
    seg_counts = lax.optimization_barrier(jnp.sum(member.astype(jnp.float32), axis=0)) * projected.shape[1]
    row_peak = lax.optimization_barrier(jnp.max(jnp.where(member, lax.optimization_barrier(jnp.max(projected, axis=1))[:, None], masked_score), axis=0))
    seg_scale = lax.rsqrt(seg_sums / seg_counts + epsilon)
    row_scale = lax.optimization_barrier(jnp.sum(jnp.where(member, seg_scale[None, :], 0.0), axis=1))
    normed = (projected * row_scale[:, None]).astype(jnp.bfloat16)
    return (normed, row_peak * seg_scale)
```

```python
import jax
import jax.numpy as jnp
from jax import lax
from jax.sharding import PartitionSpec as P

HEAD = 128


masked_score = -1e30
epsilon = 1e-06


def from_behind(x, axis, by):
    devices = lax.axis_size(axis)
    pairs = [(i, i + by) for i in range(devices) if 0 <= i + by < devices]
    return lax.ppermute(x, axis, pairs)


def key_scores(query_heads, key_heads):
    return jnp.einsum(
        "rhd,khd->hrk", query_heads, key_heads, preferred_element_type=jnp.float32
    ) * HEAD ** (-0.5)


def finish(scores, allowed, value_heads):
    scores = jnp.where(allowed[None], scores, masked_score)
    row_top = jnp.max(scores, axis=2, keepdims=True)
    exp_terms = jnp.where(allowed[None], jnp.exp(scores - row_top), 0.0)
    row_total = jnp.maximum(jnp.sum(exp_terms, axis=2), 1.0)
    weights = exp_terms.astype(jnp.bfloat16)
    mixed_out = jnp.einsum("hrk,khd->rhd", weights, value_heads, preferred_element_type=jnp.float32)
    return mixed_out / row_total.T[:, :, None]


def per_device(queries, keys, values, segment_ids, proj_weight):
    group_count = lax.axis_size("blk")
    group_index = lax.axis_index("blk")
    part_index = lax.axis_index("tp")
    row_count = queries.shape[0]
    width = queries.shape[1]
    heads_count = width // HEAD
    block_len = segment_ids.shape[0] // group_count
    own_begin = group_index * block_len
    query_segs = lax.dynamic_slice_in_dim(
        segment_ids, own_begin + part_index * row_count, row_count
    )
    own_keys, own_values = (
        lax.all_gather(keys, "tp", axis=0, tiled=True),
        lax.all_gather(values, "tp", axis=0, tiled=True),
    )
    before_keys, before_values = from_behind((own_keys, own_values), "blk", 1)
    after_keys, after_values = from_behind((own_keys, own_values), "blk", -1)

    def neighbor_segs(offset):
        target = group_index + offset
        inside = (target >= 0) & (target < group_count)
        begin_at = jnp.clip(target, 0, group_count - 1) * block_len
        return jnp.where(inside, lax.dynamic_slice_in_dim(segment_ids, begin_at, block_len), -2)

    seg_sets = (neighbor_segs(-1), neighbor_segs(0), neighbor_segs(1))
    key_sets = (before_keys, own_keys, after_keys)
    masks = [
        (query_segs[:, None] == key_segs[None, :]) & (query_segs[:, None] >= 0)
        for key_segs in seg_sets
    ]
    query_heads = queries.reshape(row_count, heads_count, HEAD)
    all_keys = jnp.concatenate(key_sets, axis=0).reshape(3 * block_len, heads_count, HEAD)
    scores = key_scores(query_heads, all_keys)
    full_mask = jnp.concatenate(masks, axis=1)
    value_heads = jnp.concatenate((before_values, own_values, after_values), axis=0).reshape(
        3 * block_len, heads_count, HEAD
    )
    attended = finish(scores, full_mask, value_heads).reshape(row_count, width).astype(jnp.bfloat16)
    merged = attended.reshape(row_count // 4, 4 * width)
    projected = jnp.dot(
        lax.all_gather(merged, "tp", axis=0, tiled=True),
        proj_weight,
        preferred_element_type=jnp.float32,
    )
    row_segs = lax.dynamic_slice_in_dim(segment_ids, own_begin, block_len)[::4]
    member = row_segs[:, None] == jnp.arange(group_count, dtype=jnp.int32)[None, :]
    squares = jnp.sum(projected * projected, axis=1)
    seg_sums = jnp.sum(jnp.where(member, squares[:, None], 0.0), axis=0)
    row_peak = jnp.max(jnp.where(member, jnp.max(projected, axis=1)[:, None], masked_score), axis=0)
    all_segs = segment_ids[::4]
    all_member = all_segs[:, None] == jnp.arange(group_count, dtype=jnp.int32)[None, :]
    seg_counts = jnp.sum(all_member.astype(jnp.float32), axis=0) * (
        projected.shape[1] * lax.axis_size("tp")
    )
    stats = lax.all_gather(jnp.stack([seg_sums, row_peak]), ("blk", "tp"), axis=0)
    seg_sums = jnp.sum(stats[:, 0], axis=0)
    row_peak = jnp.max(stats[:, 1], axis=0)
    seg_scale = lax.rsqrt(seg_sums / seg_counts + epsilon)
    row_scale = jnp.sum(jnp.where(member, seg_scale[None, :], 0.0), axis=1)
    normed = (projected * row_scale[:, None]).astype(jnp.bfloat16)
    return (normed, row_peak * seg_scale)


def solution(mesh):
    in_specs = (
        P(("blk", "tp"), None),
        P(("blk", "tp"), None),
        P(("blk", "tp"), None),
        P(),
        P(None, "tp"),
    )
    out_specs = (P("blk", "tp"), P())
    return jax.shard_map(
        per_device, mesh=mesh, in_specs=in_specs, out_specs=out_specs, check_vma=False
    )
```

```python
import jax
import jax.numpy as jnp
from jax import lax
from jax.sharding import Mesh
from jax.sharding import PartitionSpec as P

HEAD = 128


masked_score = -1e30
epsilon = 1e-06

ALL = ("blk", "x", "core")


def key_scores(query_heads, key_heads):
    return jnp.einsum(
        "rhd,khd->hrk", query_heads, key_heads, preferred_element_type=jnp.float32
    ) * HEAD ** (-0.5)


def finish(scores, allowed, value_heads):
    scores = jnp.where(allowed[None], scores, masked_score)
    row_top = jnp.max(scores, axis=2, keepdims=True)
    exp_terms = jnp.where(allowed[None], jnp.exp(scores - row_top), 0.0)
    row_total = jnp.maximum(jnp.sum(exp_terms, axis=2), 1.0)
    weights = exp_terms.astype(jnp.bfloat16)
    mixed_out = jnp.einsum("hrk,khd->rhd", weights, value_heads, preferred_element_type=jnp.float32)
    return mixed_out / row_total.T[:, :, None]


def shifted(x, axis, by):
    n = lax.axis_size(axis)
    return lax.ppermute(x, axis, [(i, i + by) for i in range(n) if 0 <= i + by < n])


def cyclic(x, axis, by):
    n = lax.axis_size(axis)
    return lax.ppermute(x, axis, [(i, (i + by) % n) for i in range(n)])


def butterfly(sums, peaks):
    n = 1
    for name in ALL:
        n *= lax.axis_size(name)
    bit = 1
    while bit < n:
        perm = [(i, i ^ bit) for i in range(n)]
        other_sums, other_peaks = lax.ppermute((sums, peaks), ALL, perm)
        sums = sums + other_sums
        peaks = jnp.maximum(peaks, other_peaks)
        bit *= 2
    return sums, peaks


def per_device(queries, keys, values, segment_ids, proj_weight):
    group_count = lax.axis_size("blk")
    chips = lax.axis_size("x")
    cores = lax.axis_size("core")
    b = lax.axis_index("blk")
    xi = lax.axis_index("x")
    c = lax.axis_index("core")
    row_count, width = queries.shape
    heads_count = width // HEAD
    slot_heads = -(-heads_count // cores)
    slot = slot_heads * HEAD
    block_len = segment_ids.shape[0] // group_count
    chunk = row_count * cores
    chip_begin = b * block_len + xi * chunk

    my_col = c * (width - slot)
    sib_col = (1 - c) * (width - slot)

    def cols(a, at):
        return lax.dynamic_slice_in_dim(a, at, slot, axis=1)

    own = jnp.concatenate([cols(queries, my_col), cols(keys, my_col), cols(values, my_col)], axis=1)
    give = jnp.concatenate([cols(queries, sib_col), cols(keys, sib_col), cols(values, sib_col)], axis=1)
    got = cyclic(give, "core", 1)
    first = c == 0
    chip_rows = jnp.concatenate(
        [jnp.where(first, own, got), jnp.where(first, got, own)], axis=0
    )
    q_chip = chip_rows[:, :slot]
    kv_chip = chip_rows[:, slot:]

    kv_block = lax.all_gather(kv_chip, "x", axis=0, tiled=True)
    kv_prev = shifted(kv_chip, "blk", 1)
    kv_next = shifted(kv_chip, "blk", -1)

    padded_segs = jnp.concatenate(
        [jnp.full((block_len,), -2, jnp.int32), segment_ids, jnp.full((block_len,), -2, jnp.int32)]
    )

    def segs_at(begin, length):
        return lax.dynamic_slice_in_dim(padded_segs, begin + block_len, length)

    kv_sets = [kv_block, kv_prev, kv_next]
    seg_sets = [
        segs_at(b * block_len, block_len),
        segs_at((b - 1) * block_len + xi * chunk, chunk),
        segs_at((b + 1) * block_len + xi * chunk, chunk),
    ]
    for s in range(1, chips):
        send = jnp.where(xi >= s, kv_prev, kv_next)
        kv_sets.append(cyclic(send, "x", -s))
        src = xi + s
        begin = jnp.where(
            src < chips,
            (b - 1) * block_len + src * chunk,
            (b + 1) * block_len + (src - chips) * chunk,
        )
        seg_sets.append(segs_at(begin, chunk))

    query_segs = lax.dynamic_slice_in_dim(segment_ids, chip_begin, chunk)
    key_segs = jnp.concatenate(seg_sets)
    all_kv = jnp.concatenate(kv_sets, axis=0)
    key_total = all_kv.shape[0]
    allowed = (query_segs[:, None] == key_segs[None, :]) & (query_segs[:, None] >= 0)
    query_heads = q_chip.reshape(chunk, slot_heads, HEAD)
    key_heads = all_kv[:, :slot].reshape(key_total, slot_heads, HEAD)
    value_heads = all_kv[:, slot:].reshape(key_total, slot_heads, HEAD)
    scores = key_scores(query_heads, key_heads)
    mixed = finish(scores, allowed, value_heads).reshape(chunk, slot).astype(jnp.bfloat16)

    mine = lax.dynamic_slice_in_dim(mixed, c * row_count, row_count)
    theirs = lax.dynamic_slice_in_dim(mixed, (1 - c) * row_count, row_count)
    back = cyclic(theirs, "core", 1)
    overlap = 2 * slot - width
    attended = jnp.where(
        first,
        jnp.concatenate([mine, back[:, overlap:]], axis=1),
        jnp.concatenate([back[:, : width - slot], mine], axis=1),
    )

    merged = attended.reshape(row_count // 4, 4 * width)
    projected = jnp.dot(
        lax.all_gather(merged, ("x", "core"), axis=0, tiled=True),
        proj_weight,
        preferred_element_type=jnp.float32,
    )
    own_begin = b * block_len
    row_segs = lax.dynamic_slice_in_dim(segment_ids, own_begin, block_len)[::4]
    member = row_segs[:, None] == jnp.arange(group_count, dtype=jnp.int32)[None, :]
    squares = jnp.sum(projected * projected, axis=1)
    seg_sums = jnp.sum(jnp.where(member, squares[:, None], 0.0), axis=0)
    row_peak = jnp.max(jnp.where(member, jnp.max(projected, axis=1)[:, None], masked_score), axis=0)
    all_segs = segment_ids[::4]
    all_member = all_segs[:, None] == jnp.arange(group_count, dtype=jnp.int32)[None, :]
    seg_counts = jnp.sum(all_member.astype(jnp.float32), axis=0) * (
        projected.shape[1] * chips * cores
    )
    seg_sums, row_peak = butterfly(seg_sums, row_peak)
    seg_scale = lax.rsqrt(seg_sums / seg_counts + epsilon)
    row_scale = jnp.sum(jnp.where(member, seg_scale[None, :], 0.0), axis=1)
    normed = (projected * row_scale[:, None]).astype(jnp.bfloat16)
    return (normed, row_peak * seg_scale)


def solution(mesh):
    blk, tp = mesh.devices.shape
    cores = 2
    chip_mesh = Mesh(mesh.devices.reshape(blk, tp // cores, cores), ALL)
    rows = P(ALL, None)
    in_specs = (rows, rows, rows, P(), P(None, ("x", "core")))
    out_specs = (P("blk", ("x", "core")), P())
    return jax.shard_map(
        per_device, mesh=chip_mesh, in_specs=in_specs, out_specs=out_specs, check_vma=False
    )
```

```python
import jax
import jax.numpy as jnp
from jax import lax
from jax.sharding import Mesh
from jax.sharding import PartitionSpec as P

HEAD = 128


masked_score = -1e30
epsilon = 1e-06

ALL = ("blk", "x", "core")


def key_scores(query_heads, key_heads):
    return jnp.einsum(
        "rhd,khd->hrk", query_heads, key_heads, preferred_element_type=jnp.float32
    ) * HEAD ** (-0.5)


def finish(scores, allowed, value_heads):
    scores = jnp.where(allowed[None], scores, masked_score)
    row_top = jnp.max(scores, axis=2, keepdims=True)
    exp_terms = jnp.where(allowed[None], jnp.exp(scores - row_top), 0.0)
    row_total = jnp.maximum(jnp.sum(exp_terms, axis=2), 1.0)
    weights = exp_terms.astype(jnp.bfloat16)
    mixed_out = jnp.einsum("hrk,khd->rhd", weights, value_heads, preferred_element_type=jnp.float32)
    return mixed_out / row_total.T[:, :, None]


def shifted(x, axis, by):
    n = lax.axis_size(axis)
    return lax.ppermute(x, axis, [(i, i + by) for i in range(n) if 0 <= i + by < n])


def cyclic(x, axis, by):
    n = lax.axis_size(axis)
    return lax.ppermute(x, axis, [(i, (i + by) % n) for i in range(n)])


def butterfly(sums, peaks):
    n = 1
    for name in ALL:
        n *= lax.axis_size(name)
    bit = 1
    while bit < n:
        perm = [(i, i ^ bit) for i in range(n)]
        other = lax.ppermute(jnp.stack([sums, peaks]), ALL, perm)
        sums = sums + other[0]
        peaks = jnp.maximum(peaks, other[1])
        bit *= 2
    return sums, peaks


def per_device(queries, keys, values, segment_ids, proj_weight):
    group_count = lax.axis_size("blk")
    chips = lax.axis_size("x")
    cores = lax.axis_size("core")
    b = lax.axis_index("blk")
    xi = lax.axis_index("x")
    c = lax.axis_index("core")
    row_count, width = queries.shape
    heads_count = width // HEAD
    slot_heads = -(-heads_count // cores)
    slot = slot_heads * HEAD
    block_len = segment_ids.shape[0] // group_count
    chunk = row_count * cores
    chip_begin = b * block_len + xi * chunk

    my_col = c * (width - slot)
    sib_col = (1 - c) * (width - slot)

    def cols(a, at):
        return lax.dynamic_slice_in_dim(a, at, slot, axis=1)

    own = jnp.concatenate([cols(queries, my_col), cols(keys, my_col), cols(values, my_col)], axis=1)
    give = jnp.concatenate([cols(queries, sib_col), cols(keys, sib_col), cols(values, sib_col)], axis=1)
    got = cyclic(give, "core", 1)
    first = c == 0
    chip_rows = jnp.concatenate(
        [jnp.where(first, own, got), jnp.where(first, got, own)], axis=0
    )
    q_chip = chip_rows[:, :slot]
    kv_chip = chip_rows[:, slot:]

    kv_block = lax.all_gather(kv_chip, "x", axis=0, tiled=True)
    kv_prev = shifted(kv_chip, "blk", 1)
    kv_next = shifted(kv_chip, "blk", -1)

    padded_segs = jnp.concatenate(
        [jnp.full((block_len,), -2, jnp.int32), segment_ids, jnp.full((block_len,), -2, jnp.int32)]
    )

    def segs_at(begin, length):
        return lax.dynamic_slice_in_dim(padded_segs, begin + block_len, length)

    kv_sets = [kv_block, kv_prev, kv_next]
    seg_sets = [
        segs_at(b * block_len, block_len),
        segs_at((b - 1) * block_len + xi * chunk, chunk),
        segs_at((b + 1) * block_len + xi * chunk, chunk),
    ]
    half = chips // 2
    far = lax.dynamic_slice_in_dim(kv_block, ((xi + half) % chips) * chunk, chunk)
    pairs = []
    for bb in range(group_count):
        for xx in range(chips):
            for cc in range(cores):
                to = bb + 1 if xx < half else bb - 1
                if 0 <= to < group_count:
                    pairs.append(((bb * chips + xx) * cores + cc, (to * chips + xx) * cores + cc))
    kv_sets.append(lax.ppermute(far, ALL, pairs))
    seg_sets.append(
        segs_at(
            jnp.where(
                xi < half,
                (b - 1) * block_len + (xi + half) * chunk,
                (b + 1) * block_len + (xi - half) * chunk,
            ),
            chunk,
        )
    )
    for s in (1, chips - 1):
        send = jnp.where(xi >= s, kv_prev, kv_next)
        kv_sets.append(cyclic(send, "x", -s))
        src = xi + s
        begin = jnp.where(
            src < chips,
            (b - 1) * block_len + src * chunk,
            (b + 1) * block_len + (src - chips) * chunk,
        )
        seg_sets.append(segs_at(begin, chunk))

    query_segs = lax.dynamic_slice_in_dim(segment_ids, chip_begin, chunk)
    key_segs = jnp.concatenate(seg_sets)
    all_kv = jnp.concatenate(kv_sets, axis=0)
    key_total = all_kv.shape[0]
    allowed = (query_segs[:, None] == key_segs[None, :]) & (query_segs[:, None] >= 0)
    query_heads = q_chip.reshape(chunk, slot_heads, HEAD)
    key_heads = all_kv[:, :slot].reshape(key_total, slot_heads, HEAD)
    value_heads = all_kv[:, slot:].reshape(key_total, slot_heads, HEAD)
    scores = key_scores(query_heads, key_heads)
    mixed = finish(scores, allowed, value_heads).reshape(chunk, slot).astype(jnp.bfloat16)

    mine = lax.dynamic_slice_in_dim(mixed, c * row_count, row_count)
    theirs = lax.dynamic_slice_in_dim(mixed, (1 - c) * row_count, row_count)
    back = cyclic(theirs, "core", 1)
    overlap = 2 * slot - width
    attended = jnp.where(
        first,
        jnp.concatenate([mine, back[:, overlap:]], axis=1),
        jnp.concatenate([back[:, : width - slot], mine], axis=1),
    )

    merged = attended.reshape(row_count // 4, 4 * width)
    projected = jnp.dot(
        lax.all_gather(merged, ("x", "core"), axis=0, tiled=True),
        proj_weight,
        preferred_element_type=jnp.float32,
    )
    own_begin = b * block_len
    row_segs = lax.dynamic_slice_in_dim(segment_ids, own_begin, block_len)[::4]
    member = row_segs[:, None] == jnp.arange(group_count, dtype=jnp.int32)[None, :]
    squares = jnp.sum(projected * projected, axis=1)
    seg_sums = jnp.sum(jnp.where(member, squares[:, None], 0.0), axis=0)
    row_peak = jnp.max(jnp.where(member, jnp.max(projected, axis=1)[:, None], masked_score), axis=0)
    all_segs = segment_ids[::4]
    all_member = all_segs[:, None] == jnp.arange(group_count, dtype=jnp.int32)[None, :]
    seg_counts = jnp.sum(all_member.astype(jnp.float32), axis=0) * (
        projected.shape[1] * chips * cores
    )
    seg_sums, row_peak = butterfly(seg_sums, row_peak)
    seg_scale = lax.rsqrt(seg_sums / seg_counts + epsilon)
    row_scale = jnp.sum(jnp.where(member, seg_scale[None, :], 0.0), axis=1)
    normed = (projected * row_scale[:, None]).astype(jnp.bfloat16)
    return (normed, row_peak * seg_scale)


def solution(mesh):
    blk, tp = mesh.devices.shape
    cores = 2
    chip_mesh = Mesh(mesh.devices.reshape(blk, tp // cores, cores), ALL)
    rows = P(ALL, None)
    in_specs = (rows, rows, rows, P(), P(None, ("x", "core")))
    out_specs = (P("blk", ("x", "core")), P())
    return jax.shard_map(
        per_device, mesh=chip_mesh, in_specs=in_specs, out_specs=out_specs, check_vma=False
    )
```

```python
import jax
import jax.numpy as jnp
from jax import lax
from jax.sharding import Mesh
from jax.sharding import PartitionSpec as P

HEAD = 128


masked_score = -1e30
epsilon = 1e-06

ALL = ("blk", "x", "core")


def key_scores(query_heads, key_heads):
    return jnp.einsum(
        "rhd,khd->hrk", query_heads, key_heads, preferred_element_type=jnp.float32
    ) * HEAD ** (-0.5)


def finish(scores, allowed, value_heads):
    scores = jnp.where(allowed[None], scores, masked_score)
    row_top = jnp.max(scores, axis=2, keepdims=True)
    exp_terms = jnp.where(allowed[None], jnp.exp(scores - row_top), 0.0)
    row_total = jnp.maximum(jnp.sum(exp_terms, axis=2), 1.0)
    weights = exp_terms.astype(jnp.bfloat16)
    mixed_out = jnp.einsum("hrk,khd->rhd", weights, value_heads, preferred_element_type=jnp.float32)
    return mixed_out / row_total.T[:, :, None]


def shifted(x, axis, by):
    n = lax.axis_size(axis)
    return lax.ppermute(x, axis, [(i, i + by) for i in range(n) if 0 <= i + by < n])


def cyclic(x, axis, by):
    n = lax.axis_size(axis)
    return lax.ppermute(x, axis, [(i, (i + by) % n) for i in range(n)])


def butterfly(sums, peaks):
    n = 1
    for name in ALL:
        n *= lax.axis_size(name)
    bit = 1
    while bit < n:
        perm = [(i, i ^ bit) for i in range(n)]
        other = lax.ppermute(jnp.stack([sums, peaks]), ALL, perm)
        sums = sums + other[0]
        peaks = jnp.maximum(peaks, other[1])
        bit *= 2
    return sums, peaks


def per_device(queries, keys, values, segment_ids, proj_weight):
    group_count = lax.axis_size("blk")
    chips = lax.axis_size("x")
    cores = lax.axis_size("core")
    b = lax.axis_index("blk")
    xi = lax.axis_index("x")
    c = lax.axis_index("core")
    row_count, width = queries.shape
    heads_count = width // HEAD
    slot_heads = -(-heads_count // cores)
    slot = slot_heads * HEAD
    block_len = segment_ids.shape[0] // group_count
    chunk = row_count * cores
    chip_begin = b * block_len + xi * chunk

    my_col = c * (width - slot)
    sib_col = (1 - c) * (width - slot)

    def cols(a, at):
        return lax.dynamic_slice_in_dim(a, at, slot, axis=1)

    own = jnp.concatenate([cols(queries, my_col), cols(keys, my_col), cols(values, my_col)], axis=1)
    give = jnp.concatenate([cols(queries, sib_col), cols(keys, sib_col), cols(values, sib_col)], axis=1)
    got = cyclic(give, "core", 1)
    first = c == 0
    chip_rows = jnp.concatenate(
        [jnp.where(first, own, got), jnp.where(first, got, own)], axis=0
    )
    q_chip = chip_rows[:, :slot]
    kv_chip = chip_rows[:, slot:]

    from_right = cyclic(kv_chip, "x", -1)
    from_left = cyclic(kv_chip, "x", 1)
    relay = jnp.concatenate(
        [cyclic(from_right[: row_count], "x", -1), cyclic(from_left[row_count:], "x", 1)], axis=0
    )
    kv_prev = shifted(kv_chip, "blk", 1)
    kv_next = shifted(kv_chip, "blk", -1)

    padded_segs = jnp.concatenate(
        [jnp.full((block_len,), -2, jnp.int32), segment_ids, jnp.full((block_len,), -2, jnp.int32)]
    )

    def segs_at(begin, length):
        return lax.dynamic_slice_in_dim(padded_segs, begin + block_len, length)

    kv_sets = [kv_chip, from_right, from_left, relay, kv_prev, kv_next]
    seg_sets = [
        segs_at(b * block_len + xi * chunk, chunk),
        segs_at(b * block_len + ((xi + 1) % chips) * chunk, chunk),
        segs_at(b * block_len + ((xi + chips - 1) % chips) * chunk, chunk),
        segs_at(b * block_len + ((xi + 2) % chips) * chunk, chunk),
        segs_at((b - 1) * block_len + xi * chunk, chunk),
        segs_at((b + 1) * block_len + xi * chunk, chunk),
    ]
    half = chips // 2
    far = relay
    pairs = []
    for bb in range(group_count):
        for xx in range(chips):
            for cc in range(cores):
                to = bb + 1 if xx < half else bb - 1
                if 0 <= to < group_count:
                    pairs.append(((bb * chips + xx) * cores + cc, (to * chips + xx) * cores + cc))
    kv_sets.append(lax.ppermute(far, ALL, pairs))
    seg_sets.append(
        segs_at(
            jnp.where(
                xi < half,
                (b - 1) * block_len + (xi + half) * chunk,
                (b + 1) * block_len + (xi - half) * chunk,
            ),
            chunk,
        )
    )
    for s in (1, chips - 1):
        send = jnp.where(xi >= s, kv_prev, kv_next)
        kv_sets.append(cyclic(send, "x", -s))
        src = xi + s
        begin = jnp.where(
            src < chips,
            (b - 1) * block_len + src * chunk,
            (b + 1) * block_len + (src - chips) * chunk,
        )
        seg_sets.append(segs_at(begin, chunk))

    query_segs = lax.dynamic_slice_in_dim(segment_ids, chip_begin, chunk)
    key_segs = jnp.concatenate(seg_sets)
    all_kv = jnp.concatenate(kv_sets, axis=0)
    key_total = all_kv.shape[0]
    allowed = (query_segs[:, None] == key_segs[None, :]) & (query_segs[:, None] >= 0)
    query_heads = q_chip.reshape(chunk, slot_heads, HEAD)
    key_heads = all_kv[:, :slot].reshape(key_total, slot_heads, HEAD)
    value_heads = all_kv[:, slot:].reshape(key_total, slot_heads, HEAD)
    scores = key_scores(query_heads, key_heads)
    mixed = finish(scores, allowed, value_heads).reshape(chunk, slot).astype(jnp.bfloat16)

    mine = lax.dynamic_slice_in_dim(mixed, c * row_count, row_count)
    theirs = lax.dynamic_slice_in_dim(mixed, (1 - c) * row_count, row_count)
    back = cyclic(theirs, "core", 1)
    overlap = 2 * slot - width
    attended = jnp.where(
        first,
        jnp.concatenate([mine, back[:, overlap:]], axis=1),
        jnp.concatenate([back[:, : width - slot], mine], axis=1),
    )

    merged = attended.reshape(row_count // 4, 4 * width)
    projected = jnp.dot(
        lax.all_gather(merged, ("x", "core"), axis=0, tiled=True),
        proj_weight,
        preferred_element_type=jnp.float32,
    )
    own_begin = b * block_len
    row_segs = lax.dynamic_slice_in_dim(segment_ids, own_begin, block_len)[::4]
    member = row_segs[:, None] == jnp.arange(group_count, dtype=jnp.int32)[None, :]
    squares = jnp.sum(projected * projected, axis=1)
    seg_sums = jnp.sum(jnp.where(member, squares[:, None], 0.0), axis=0)
    row_peak = jnp.max(jnp.where(member, jnp.max(projected, axis=1)[:, None], masked_score), axis=0)
    all_segs = segment_ids[::4]
    all_member = all_segs[:, None] == jnp.arange(group_count, dtype=jnp.int32)[None, :]
    seg_counts = jnp.sum(all_member.astype(jnp.float32), axis=0) * (
        projected.shape[1] * chips * cores
    )
    seg_sums, row_peak = butterfly(seg_sums, row_peak)
    seg_scale = lax.rsqrt(seg_sums / seg_counts + epsilon)
    row_scale = jnp.sum(jnp.where(member, seg_scale[None, :], 0.0), axis=1)
    normed = (projected * row_scale[:, None]).astype(jnp.bfloat16)
    return (normed, row_peak * seg_scale)


def solution(mesh):
    blk, tp = mesh.devices.shape
    cores = 2
    chip_mesh = Mesh(mesh.devices.reshape(blk, tp // cores, cores), ALL)
    rows = P(ALL, None)
    in_specs = (rows, rows, rows, P(), P(None, ("x", "core")))
    out_specs = (P("blk", ("x", "core")), P())
    return jax.shard_map(
        per_device, mesh=chip_mesh, in_specs=in_specs, out_specs=out_specs, check_vma=False
    )
```

```python
import jax
import jax.numpy as jnp
from jax import lax
from jax.sharding import Mesh
from jax.sharding import PartitionSpec as P

HEAD = 128


masked_score = -1e30
epsilon = 1e-06

ALL = ("blk", "x", "core")


def key_scores(query_heads, key_heads):
    return jnp.einsum(
        "rhd,khd->hrk", query_heads, key_heads, preferred_element_type=jnp.float32
    ) * HEAD ** (-0.5)


def finish(scores, allowed, value_heads):
    scores = jnp.where(allowed[None], scores, masked_score)
    row_top = jnp.max(scores, axis=2, keepdims=True)
    exp_terms = jnp.where(allowed[None], jnp.exp(scores - row_top), 0.0)
    row_total = jnp.maximum(jnp.sum(exp_terms, axis=2), 1.0)
    weights = exp_terms.astype(jnp.bfloat16)
    mixed_out = jnp.einsum("hrk,khd->rhd", weights, value_heads, preferred_element_type=jnp.float32)
    return mixed_out / row_total.T[:, :, None]


def shifted(x, axis, by):
    n = lax.axis_size(axis)
    return lax.ppermute(x, axis, [(i, i + by) for i in range(n) if 0 <= i + by < n])


def cyclic(x, axis, by):
    n = lax.axis_size(axis)
    return lax.ppermute(x, axis, [(i, (i + by) % n) for i in range(n)])


def butterfly(sums, peaks):
    n = 1
    for name in ALL:
        n *= lax.axis_size(name)
    bit = 1
    while bit < n:
        perm = [(i, i ^ bit) for i in range(n)]
        other = lax.ppermute(jnp.stack([sums, peaks]), ALL, perm)
        sums = sums + other[0]
        peaks = jnp.maximum(peaks, other[1])
        bit *= 2
    return sums, peaks


def per_device(queries, keys, values, segment_ids, proj_weight):
    group_count = lax.axis_size("blk")
    chips = lax.axis_size("x")
    cores = lax.axis_size("core")
    b = lax.axis_index("blk")
    xi = lax.axis_index("x")
    c = lax.axis_index("core")
    row_count, width = queries.shape
    heads_count = width // HEAD
    slot_heads = -(-heads_count // cores)
    slot = slot_heads * HEAD
    block_len = segment_ids.shape[0] // group_count
    chunk = row_count * cores
    chip_begin = b * block_len + xi * chunk

    my_col = c * (width - slot)
    sib_col = (1 - c) * (width - slot)

    def cols(a, at):
        return lax.dynamic_slice_in_dim(a, at, slot, axis=1)

    own = jnp.concatenate([cols(queries, my_col), cols(keys, my_col), cols(values, my_col)], axis=1)
    give = jnp.concatenate([cols(queries, sib_col), cols(keys, sib_col), cols(values, sib_col)], axis=1)
    got = cyclic(give, "core", 1)
    first = c == 0
    chip_rows = jnp.concatenate(
        [jnp.where(first, own, got), jnp.where(first, got, own)], axis=0
    )
    q_chip = chip_rows[:, :slot]
    kv_chip = chip_rows[:, slot:]

    from_right = cyclic(kv_chip, "x", -1)
    from_left = cyclic(kv_chip, "x", 1)
    relay = jnp.concatenate(
        [cyclic(from_right[: row_count], "x", -1), cyclic(from_left[row_count:], "x", 1)], axis=0
    )
    kv_prev = shifted(kv_chip, "blk", 1)
    kv_next = shifted(kv_chip, "blk", -1)

    padded_segs = jnp.concatenate(
        [jnp.full((block_len,), -2, jnp.int32), segment_ids, jnp.full((block_len,), -2, jnp.int32)]
    )

    def segs_at(begin, length):
        return lax.dynamic_slice_in_dim(padded_segs, begin + block_len, length)

    kv_sets = [kv_chip, from_right, from_left, relay, kv_prev, kv_next]
    seg_sets = [
        segs_at(b * block_len + xi * chunk, chunk),
        segs_at(b * block_len + ((xi + 1) % chips) * chunk, chunk),
        segs_at(b * block_len + ((xi + chips - 1) % chips) * chunk, chunk),
        segs_at(b * block_len + ((xi + 2) % chips) * chunk, chunk),
        segs_at((b - 1) * block_len + xi * chunk, chunk),
        segs_at((b + 1) * block_len + xi * chunk, chunk),
    ]
    half = chips // 2
    far = relay
    pairs = []
    for bb in range(group_count):
        for xx in range(chips):
            for cc in range(cores):
                to = bb + 1 if xx < half else bb - 1
                if 0 <= to < group_count:
                    pairs.append(((bb * chips + xx) * cores + cc, (to * chips + xx) * cores + cc))
    kv_sets.append(lax.ppermute(far, ALL, pairs))
    seg_sets.append(
        segs_at(
            jnp.where(
                xi < half,
                (b - 1) * block_len + (xi + half) * chunk,
                (b + 1) * block_len + (xi - half) * chunk,
            ),
            chunk,
        )
    )
    for s in (1, chips - 1):
        send = jnp.where(xi >= s, kv_prev, kv_next)
        kv_sets.append(cyclic(send, "x", -s))
        src = xi + s
        begin = jnp.where(
            src < chips,
            (b - 1) * block_len + src * chunk,
            (b + 1) * block_len + (src - chips) * chunk,
        )
        seg_sets.append(segs_at(begin, chunk))

    query_segs = lax.dynamic_slice_in_dim(segment_ids, chip_begin, chunk)
    key_segs = jnp.concatenate(seg_sets)
    all_kv = jnp.concatenate(kv_sets, axis=0)
    key_total = all_kv.shape[0]
    allowed = (query_segs[:, None] == key_segs[None, :]) & (query_segs[:, None] >= 0)
    query_heads = q_chip.reshape(chunk, slot_heads, HEAD)
    key_heads = all_kv[:, :slot].reshape(key_total, slot_heads, HEAD)
    value_heads = all_kv[:, slot:].reshape(key_total, slot_heads, HEAD)
    scores = key_scores(query_heads, key_heads)
    mixed = finish(scores, allowed, value_heads).reshape(chunk, slot).astype(jnp.bfloat16)

    mine = lax.dynamic_slice_in_dim(mixed, c * row_count, row_count)
    theirs = lax.dynamic_slice_in_dim(mixed, (1 - c) * row_count, row_count)
    back = cyclic(theirs, "core", 1)
    overlap = 2 * slot - width
    attended = jnp.where(
        first,
        jnp.concatenate([mine, back[:, overlap:]], axis=1),
        jnp.concatenate([back[:, : width - slot], mine], axis=1),
    )

    merged = attended.reshape(row_count // 4, 4 * width)
    piece = merged.shape[0]
    m_right = cyclic(merged, "x", -1)
    m_left = cyclic(merged, "x", 1)
    m_far = jnp.concatenate(
        [cyclic(m_right[: piece // 2], "x", -1), cyclic(m_left[piece // 2 :], "x", 1)], axis=0
    )
    mine4 = jnp.stack([merged, m_right, m_left, m_far])
    sib4 = cyclic(mine4, "core", 1)
    gathered = jnp.zeros((piece * chips * cores, merged.shape[1]), merged.dtype)
    for k, dx in enumerate((0, 1, chips - 1, 2)):
        at = (xi + dx) % chips
        gathered = lax.dynamic_update_slice_in_dim(gathered, mine4[k], (at * cores + c) * piece, 0)
        gathered = lax.dynamic_update_slice_in_dim(gathered, sib4[k], (at * cores + 1 - c) * piece, 0)
    projected = jnp.dot(gathered, proj_weight, preferred_element_type=jnp.float32)
    own_begin = b * block_len
    row_segs = lax.dynamic_slice_in_dim(segment_ids, own_begin, block_len)[::4]
    member = row_segs[:, None] == jnp.arange(group_count, dtype=jnp.int32)[None, :]
    squares = jnp.sum(projected * projected, axis=1)
    seg_sums = jnp.sum(jnp.where(member, squares[:, None], 0.0), axis=0)
    row_peak = jnp.max(jnp.where(member, jnp.max(projected, axis=1)[:, None], masked_score), axis=0)
    all_segs = segment_ids[::4]
    all_member = all_segs[:, None] == jnp.arange(group_count, dtype=jnp.int32)[None, :]
    seg_counts = jnp.sum(all_member.astype(jnp.float32), axis=0) * (
        projected.shape[1] * chips * cores
    )
    seg_sums, row_peak = butterfly(seg_sums, row_peak)
    seg_scale = lax.rsqrt(seg_sums / seg_counts + epsilon)
    row_scale = jnp.sum(jnp.where(member, seg_scale[None, :], 0.0), axis=1)
    normed = (projected * row_scale[:, None]).astype(jnp.bfloat16)
    return (normed, row_peak * seg_scale)


def solution(mesh):
    blk, tp = mesh.devices.shape
    cores = 2
    chip_mesh = Mesh(mesh.devices.reshape(blk, tp // cores, cores), ALL)
    rows = P(ALL, None)
    in_specs = (rows, rows, rows, P(), P(None, ("x", "core")))
    out_specs = (P("blk", ("x", "core")), P())
    return jax.shard_map(
        per_device, mesh=chip_mesh, in_specs=in_specs, out_specs=out_specs, check_vma=False
    )
```

```python
import jax
import jax.numpy as jnp
from jax import lax
from jax.sharding import Mesh
from jax.sharding import PartitionSpec as P

HEAD = 128


masked_score = -1e30
epsilon = 1e-06

ALL = ("blk", "x", "core")


def key_scores(query_heads, key_heads):
    return jnp.einsum(
        "rhd,khd->hrk", query_heads, key_heads, preferred_element_type=jnp.float32
    ) * HEAD ** (-0.5)


def finish(scores, allowed, value_heads):
    scores = jnp.where(allowed[None], scores, masked_score)
    row_top = jnp.max(scores, axis=2, keepdims=True)
    exp_terms = jnp.where(allowed[None], jnp.exp(scores - row_top), 0.0)
    row_total = jnp.maximum(jnp.sum(exp_terms, axis=2), 1.0)
    weights = exp_terms.astype(jnp.bfloat16)
    mixed_out = jnp.einsum("hrk,khd->rhd", weights, value_heads, preferred_element_type=jnp.float32)
    return mixed_out / row_total.T[:, :, None]


def shifted(x, axis, by):
    n = lax.axis_size(axis)
    return lax.ppermute(x, axis, [(i, i + by) for i in range(n) if 0 <= i + by < n])


def cyclic(x, axis, by):
    n = lax.axis_size(axis)
    return lax.ppermute(x, axis, [(i, (i + by) % n) for i in range(n)])


def butterfly(sums, peaks):
    n = 1
    for name in ALL:
        n *= lax.axis_size(name)
    bit = 1
    while bit < n:
        perm = [(i, i ^ bit) for i in range(n)]
        other = lax.ppermute(jnp.stack([sums, peaks]), ALL, perm)
        sums = sums + other[0]
        peaks = jnp.maximum(peaks, other[1])
        bit *= 2
    return sums, peaks


def per_device(queries, keys, values, segment_ids, proj_weight):
    group_count = lax.axis_size("blk")
    chips = lax.axis_size("x")
    cores = lax.axis_size("core")
    b = lax.axis_index("blk")
    xi = lax.axis_index("x")
    c = lax.axis_index("core")
    row_count, width = queries.shape
    heads_count = width // HEAD
    slot_heads = -(-heads_count // cores)
    slot = slot_heads * HEAD
    block_len = segment_ids.shape[0] // group_count
    chunk = row_count * cores
    chip_begin = b * block_len + xi * chunk

    my_col = c * (width - slot)
    sib_col = (1 - c) * (width - slot)

    def cols(a, at):
        return lax.dynamic_slice_in_dim(a, at, slot, axis=1)

    own = jnp.concatenate([cols(queries, my_col), cols(keys, my_col), cols(values, my_col)], axis=1)
    give = jnp.concatenate([cols(queries, sib_col), cols(keys, sib_col), cols(values, sib_col)], axis=1)
    got = cyclic(give, "core", 1)
    first = c == 0
    chip_rows = jnp.concatenate(
        [jnp.where(first, own, got), jnp.where(first, got, own)], axis=0
    )
    q_chip = chip_rows[:, :slot]
    kv_chip = chip_rows[:, slot:]

    from_right = cyclic(kv_chip, "x", -1)
    from_left = cyclic(kv_chip, "x", 1)
    relay = jnp.concatenate(
        [cyclic(from_right[: row_count], "x", -1), cyclic(from_left[row_count:], "x", 1)], axis=0
    )
    kv_prev = shifted(kv_chip, "blk", 1)
    kv_next = shifted(kv_chip, "blk", -1)

    padded_segs = jnp.concatenate(
        [jnp.full((block_len,), -2, jnp.int32), segment_ids, jnp.full((block_len,), -2, jnp.int32)]
    )

    def segs_at(begin, length):
        return lax.dynamic_slice_in_dim(padded_segs, begin + block_len, length)

    kv_sets = [kv_chip, from_right, from_left, relay, kv_prev, kv_next]
    seg_sets = [
        segs_at(b * block_len + xi * chunk, chunk),
        segs_at(b * block_len + ((xi + 1) % chips) * chunk, chunk),
        segs_at(b * block_len + ((xi + chips - 1) % chips) * chunk, chunk),
        segs_at(b * block_len + ((xi + 2) % chips) * chunk, chunk),
        segs_at((b - 1) * block_len + xi * chunk, chunk),
        segs_at((b + 1) * block_len + xi * chunk, chunk),
    ]
    half = chips // 2
    far = relay
    pairs = []
    for bb in range(group_count):
        for xx in range(chips):
            for cc in range(cores):
                to = bb + 1 if xx < half else bb - 1
                if 0 <= to < group_count:
                    pairs.append(((bb * chips + xx) * cores + cc, (to * chips + xx) * cores + cc))
    kv_sets.append(lax.ppermute(far, ALL, pairs))
    seg_sets.append(
        segs_at(
            jnp.where(
                xi < half,
                (b - 1) * block_len + (xi + half) * chunk,
                (b + 1) * block_len + (xi - half) * chunk,
            ),
            chunk,
        )
    )
    for s in (1, chips - 1):
        send = jnp.where(xi >= s, kv_prev, kv_next)
        kv_sets.append(cyclic(send, "x", -s))
        src = xi + s
        begin = jnp.where(
            src < chips,
            (b - 1) * block_len + src * chunk,
            (b + 1) * block_len + (src - chips) * chunk,
        )
        seg_sets.append(segs_at(begin, chunk))

    query_segs = lax.dynamic_slice_in_dim(segment_ids, chip_begin, chunk)
    key_segs = jnp.concatenate(seg_sets)
    all_kv = jnp.concatenate(kv_sets, axis=0)
    key_total = all_kv.shape[0]
    allowed = (query_segs[:, None] == key_segs[None, :]) & (query_segs[:, None] >= 0)
    key_heads = all_kv[:, :slot].reshape(key_total, slot_heads, HEAD)
    value_heads = all_kv[:, slot:].reshape(key_total, slot_heads, HEAD)
    overlap = 2 * slot - width
    piece = row_count // 4
    gathered = jnp.zeros((piece * chips * cores, 4 * width), queries.dtype)

    parts = 2
    part = row_count // parts
    for h in range(parts):
        pick = jnp.concatenate(
            [jnp.arange(h * part, (h + 1) * part), row_count + jnp.arange(h * part, (h + 1) * part)]
        )
        query_heads = q_chip[pick].reshape(cores * part, slot_heads, HEAD)
        scores = key_scores(query_heads, key_heads)
        mixed = finish(scores, allowed[pick], value_heads).reshape(cores * part, slot).astype(jnp.bfloat16)

        mine = lax.dynamic_slice_in_dim(mixed, c * part, part)
        theirs = lax.dynamic_slice_in_dim(mixed, (1 - c) * part, part)
        back = cyclic(theirs, "core", 1)
        attended = jnp.where(
            first,
            jnp.concatenate([mine, back[:, overlap:]], axis=1),
            jnp.concatenate([back[:, : width - slot], mine], axis=1),
        )
        merged = attended.reshape(part // 4, 4 * width)
        rows = merged.shape[0]
        m_right = cyclic(merged, "x", -1)
        m_left = cyclic(merged, "x", 1)
        m_far = jnp.concatenate(
            [cyclic(m_right[: rows // 2], "x", -1), cyclic(m_left[rows // 2 :], "x", 1)], axis=0
        )
        mine4 = jnp.stack([merged, m_right, m_left, m_far])
        sib4 = cyclic(mine4, "core", 1)
        for k, dx in enumerate((0, 1, chips - 1, 2)):
            at = (xi + dx) % chips
            gathered = lax.dynamic_update_slice_in_dim(
                gathered, mine4[k], (at * cores + c) * piece + h * rows, 0
            )
            gathered = lax.dynamic_update_slice_in_dim(
                gathered, sib4[k], (at * cores + 1 - c) * piece + h * rows, 0
            )
    projected = jnp.dot(gathered, proj_weight, preferred_element_type=jnp.float32)
    own_begin = b * block_len
    row_segs = lax.dynamic_slice_in_dim(segment_ids, own_begin, block_len)[::4]
    member = row_segs[:, None] == jnp.arange(group_count, dtype=jnp.int32)[None, :]
    squares = jnp.sum(projected * projected, axis=1)
    seg_sums = jnp.sum(jnp.where(member, squares[:, None], 0.0), axis=0)
    row_peak = jnp.max(jnp.where(member, jnp.max(projected, axis=1)[:, None], masked_score), axis=0)
    all_segs = segment_ids[::4]
    all_member = all_segs[:, None] == jnp.arange(group_count, dtype=jnp.int32)[None, :]
    seg_counts = jnp.sum(all_member.astype(jnp.float32), axis=0) * (
        projected.shape[1] * chips * cores
    )
    seg_sums, row_peak = butterfly(seg_sums, row_peak)
    seg_scale = lax.rsqrt(seg_sums / seg_counts + epsilon)
    row_scale = jnp.sum(jnp.where(member, seg_scale[None, :], 0.0), axis=1)
    normed = (projected * row_scale[:, None]).astype(jnp.bfloat16)
    return (normed, row_peak * seg_scale)


def solution(mesh):
    blk, tp = mesh.devices.shape
    cores = 2
    chip_mesh = Mesh(mesh.devices.reshape(blk, tp // cores, cores), ALL)
    rows = P(ALL, None)
    in_specs = (rows, rows, rows, P(), P(None, ("x", "core")))
    out_specs = (P("blk", ("x", "core")), P())
    return jax.shard_map(
        per_device, mesh=chip_mesh, in_specs=in_specs, out_specs=out_specs, check_vma=False
    )
```

```python
import jax
import jax.numpy as jnp
from jax import lax
from jax.sharding import Mesh
from jax.sharding import PartitionSpec as P

HEAD = 128


masked_score = -1e30
epsilon = 1e-06

ALL = ("blk", "x", "core")


def key_scores(query_heads, key_heads):
    return jnp.einsum(
        "rhd,khd->hrk", query_heads, key_heads, preferred_element_type=jnp.float32
    ) * HEAD ** (-0.5)


def finish(scores, allowed, value_heads):
    scores = jnp.where(allowed[None], scores, masked_score)
    row_top = jnp.max(scores, axis=2, keepdims=True)
    exp_terms = jnp.where(allowed[None], jnp.exp(scores - row_top), 0.0)
    row_total = jnp.maximum(jnp.sum(exp_terms, axis=2), 1.0)
    weights = exp_terms.astype(jnp.bfloat16)
    mixed_out = jnp.einsum("hrk,khd->rhd", weights, value_heads, preferred_element_type=jnp.float32)
    return mixed_out / row_total.T[:, :, None]


def shifted(x, axis, by):
    n = lax.axis_size(axis)
    return lax.ppermute(x, axis, [(i, i + by) for i in range(n) if 0 <= i + by < n])


def cyclic(x, axis, by):
    n = lax.axis_size(axis)
    return lax.ppermute(x, axis, [(i, (i + by) % n) for i in range(n)])


def butterfly(sums, peaks):
    n = 1
    for name in ALL:
        n *= lax.axis_size(name)
    bit = 1
    while bit < n:
        perm = [(i, i ^ bit) for i in range(n)]
        other = lax.ppermute(jnp.stack([sums, peaks]), ALL, perm)
        sums = sums + other[0]
        peaks = jnp.maximum(peaks, other[1])
        bit *= 2
    return sums, peaks


def per_device(queries, keys, values, segment_ids, proj_weight):
    group_count = lax.axis_size("blk")
    chips = lax.axis_size("x")
    cores = lax.axis_size("core")
    b = lax.axis_index("blk")
    xi = lax.axis_index("x")
    c = lax.axis_index("core")
    row_count, width = queries.shape
    heads_count = width // HEAD
    slot_heads = -(-heads_count // cores)
    slot = slot_heads * HEAD
    block_len = segment_ids.shape[0] // group_count
    chunk = row_count * cores
    chip_begin = b * block_len + xi * chunk

    my_col = c * (width - slot)
    sib_col = (1 - c) * (width - slot)

    def cols(a, at):
        return lax.dynamic_slice_in_dim(a, at, slot, axis=1)

    own = jnp.concatenate([cols(queries, my_col), cols(keys, my_col), cols(values, my_col)], axis=1)
    give = jnp.concatenate([cols(queries, sib_col), cols(keys, sib_col), cols(values, sib_col)], axis=1)
    got = cyclic(give, "core", 1)
    first = c == 0
    chip_rows = jnp.concatenate(
        [jnp.where(first, own, got), jnp.where(first, got, own)], axis=0
    )
    q_chip = chip_rows[:, :slot]
    kv_chip = chip_rows[:, slot:]

    from_right = cyclic(kv_chip, "x", -1)
    from_left = cyclic(kv_chip, "x", 1)
    relay_a = cyclic(from_right[:row_count], "x", -1)
    relay_b = cyclic(from_left[row_count:], "x", 1)
    relay = jnp.concatenate([relay_a, relay_b], axis=0)
    kv_prev = shifted(kv_chip, "blk", 1)
    kv_next = shifted(kv_chip, "blk", -1)

    padded_segs = jnp.concatenate(
        [jnp.full((block_len,), -2, jnp.int32), segment_ids, jnp.full((block_len,), -2, jnp.int32)]
    )

    def segs_at(begin, length):
        return lax.dynamic_slice_in_dim(padded_segs, begin + block_len, length)

    kv_sets = [kv_chip, from_right, from_left, relay, kv_prev, kv_next]
    seg_sets = [
        segs_at(b * block_len + xi * chunk, chunk),
        segs_at(b * block_len + ((xi + 1) % chips) * chunk, chunk),
        segs_at(b * block_len + ((xi + chips - 1) % chips) * chunk, chunk),
        segs_at(b * block_len + ((xi + 2) % chips) * chunk, chunk),
        segs_at((b - 1) * block_len + xi * chunk, chunk),
        segs_at((b + 1) * block_len + xi * chunk, chunk),
    ]
    half = chips // 2
    pairs = []
    for bb in range(group_count):
        for xx in range(chips):
            for cc in range(cores):
                to = bb + 1 if xx < half else bb - 1
                if 0 <= to < group_count:
                    pairs.append(((bb * chips + xx) * cores + cc, (to * chips + xx) * cores + cc))
    kv_sets.append(
        jnp.concatenate([lax.ppermute(relay_a, ALL, pairs), lax.ppermute(relay_b, ALL, pairs)], axis=0)
    )
    seg_sets.append(
        segs_at(
            jnp.where(
                xi < half,
                (b - 1) * block_len + (xi + half) * chunk,
                (b + 1) * block_len + (xi - half) * chunk,
            ),
            chunk,
        )
    )
    for s in (1, chips - 1):
        send = jnp.where(xi >= s, kv_prev, kv_next)
        kv_sets.append(cyclic(send, "x", -s))
        src = xi + s
        begin = jnp.where(
            src < chips,
            (b - 1) * block_len + src * chunk,
            (b + 1) * block_len + (src - chips) * chunk,
        )
        seg_sets.append(segs_at(begin, chunk))

    query_segs = lax.dynamic_slice_in_dim(segment_ids, chip_begin, chunk)
    key_segs = jnp.concatenate(seg_sets)
    all_kv = jnp.concatenate(kv_sets, axis=0)
    key_total = all_kv.shape[0]
    allowed = (query_segs[:, None] == key_segs[None, :]) & (query_segs[:, None] >= 0)
    query_heads = q_chip.reshape(chunk, slot_heads, HEAD)
    key_heads = all_kv[:, :slot].reshape(key_total, slot_heads, HEAD)
    value_heads = all_kv[:, slot:].reshape(key_total, slot_heads, HEAD)
    scores = key_scores(query_heads, key_heads)
    mixed = finish(scores, allowed, value_heads).reshape(chunk, slot).astype(jnp.bfloat16)

    mine = lax.dynamic_slice_in_dim(mixed, c * row_count, row_count)
    theirs = lax.dynamic_slice_in_dim(mixed, (1 - c) * row_count, row_count)
    back = cyclic(theirs, "core", 1)
    overlap = 2 * slot - width
    attended = jnp.where(
        first,
        jnp.concatenate([mine, back[:, overlap:]], axis=1),
        jnp.concatenate([back[:, : width - slot], mine], axis=1),
    )

    merged = attended.reshape(row_count // 4, 4 * width)
    piece = merged.shape[0]
    m_right = cyclic(merged, "x", -1)
    m_left = cyclic(merged, "x", 1)
    m_far = jnp.concatenate(
        [cyclic(m_right[: piece // 2], "x", -1), cyclic(m_left[piece // 2 :], "x", 1)], axis=0
    )
    mine4 = jnp.stack([merged, m_right, m_left, m_far])
    sib4 = cyclic(mine4, "core", 1)
    gathered = jnp.zeros((piece * chips * cores, merged.shape[1]), merged.dtype)
    for k, dx in enumerate((0, 1, chips - 1, 2)):
        at = (xi + dx) % chips
        gathered = lax.dynamic_update_slice_in_dim(gathered, mine4[k], (at * cores + c) * piece, 0)
        gathered = lax.dynamic_update_slice_in_dim(gathered, sib4[k], (at * cores + 1 - c) * piece, 0)
    projected = jnp.dot(gathered, proj_weight, preferred_element_type=jnp.float32)
    own_begin = b * block_len
    row_segs = lax.dynamic_slice_in_dim(segment_ids, own_begin, block_len)[::4]
    member = row_segs[:, None] == jnp.arange(group_count, dtype=jnp.int32)[None, :]
    squares = jnp.sum(projected * projected, axis=1)
    seg_sums = jnp.sum(jnp.where(member, squares[:, None], 0.0), axis=0)
    row_peak = jnp.max(jnp.where(member, jnp.max(projected, axis=1)[:, None], masked_score), axis=0)
    all_segs = segment_ids[::4]
    all_member = all_segs[:, None] == jnp.arange(group_count, dtype=jnp.int32)[None, :]
    seg_counts = jnp.sum(all_member.astype(jnp.float32), axis=0) * (
        projected.shape[1] * chips * cores
    )
    seg_sums, row_peak = butterfly(seg_sums, row_peak)
    seg_scale = lax.rsqrt(seg_sums / seg_counts + epsilon)
    row_scale = jnp.sum(jnp.where(member, seg_scale[None, :], 0.0), axis=1)
    normed = (projected * row_scale[:, None]).astype(jnp.bfloat16)
    return (normed, row_peak * seg_scale)


def solution(mesh):
    blk, tp = mesh.devices.shape
    cores = 2
    chip_mesh = Mesh(mesh.devices.reshape(blk, tp // cores, cores), ALL)
    rows = P(ALL, None)
    in_specs = (rows, rows, rows, P(), P(None, ("x", "core")))
    out_specs = (P("blk", ("x", "core")), P())
    return jax.shard_map(
        per_device, mesh=chip_mesh, in_specs=in_specs, out_specs=out_specs, check_vma=False
    )
```

```python
import jax
import jax.numpy as jnp
from jax import lax
from jax.sharding import Mesh
from jax.sharding import PartitionSpec as P

HEAD = 128


masked_score = -1e30
epsilon = 1e-06

ALL = ("blk", "x", "core")


def key_scores(query_heads, key_heads):
    return jnp.einsum(
        "rhd,khd->hrk", query_heads, key_heads, preferred_element_type=jnp.float32
    ) * HEAD ** (-0.5)


def finish(scores, allowed, value_heads):
    scores = jnp.where(allowed[None], scores, masked_score)
    row_top = jnp.max(scores, axis=2, keepdims=True)
    exp_terms = jnp.where(allowed[None], jnp.exp(scores - row_top), 0.0)
    row_total = jnp.maximum(jnp.sum(exp_terms, axis=2), 1.0)
    weights = exp_terms.astype(jnp.bfloat16)
    mixed_out = jnp.einsum("hrk,khd->rhd", weights, value_heads, preferred_element_type=jnp.float32)
    return mixed_out / row_total.T[:, :, None]


def shifted(x, axis, by):
    n = lax.axis_size(axis)
    return lax.ppermute(x, axis, [(i, i + by) for i in range(n) if 0 <= i + by < n])


def cyclic(x, axis, by):
    n = lax.axis_size(axis)
    return lax.ppermute(x, axis, [(i, (i + by) % n) for i in range(n)])


def butterfly(sums, peaks):
    n = 1
    for name in ALL:
        n *= lax.axis_size(name)
    bit = 1
    while bit < n:
        perm = [(i, i ^ bit) for i in range(n)]
        other = lax.ppermute(jnp.stack([sums, peaks]), ALL, perm)
        sums = sums + other[0]
        peaks = jnp.maximum(peaks, other[1])
        bit *= 2
    return sums, peaks


def per_device(queries, keys, values, segment_ids, proj_weight):
    group_count = lax.axis_size("blk")
    chips = lax.axis_size("x")
    cores = lax.axis_size("core")
    b = lax.axis_index("blk")
    xi = lax.axis_index("x")
    c = lax.axis_index("core")
    row_count, width = queries.shape
    heads_count = width // HEAD
    slot_heads = -(-heads_count // cores)
    slot = slot_heads * HEAD
    block_len = segment_ids.shape[0] // group_count
    chunk = row_count * cores
    chip_begin = b * block_len + xi * chunk

    my_col = c * (width - slot)
    sib_col = (1 - c) * (width - slot)

    def cols(a, at):
        return lax.dynamic_slice_in_dim(a, at, slot, axis=1)

    own = jnp.concatenate([cols(queries, my_col), cols(keys, my_col), cols(values, my_col)], axis=1)
    give = jnp.concatenate([cols(queries, sib_col), cols(keys, sib_col), cols(values, sib_col)], axis=1)
    got = cyclic(give, "core", 1)
    first = c == 0
    chip_rows = jnp.concatenate(
        [jnp.where(first, own, got), jnp.where(first, got, own)], axis=0
    )
    q_chip = chip_rows[:, :slot]
    kv_chip = chip_rows[:, slot:]

    from_right = cyclic(kv_chip, "x", -1)
    from_left = cyclic(kv_chip, "x", 1)
    relay = jnp.concatenate(
        [cyclic(from_right[: row_count], "x", -1), cyclic(from_left[row_count:], "x", 1)], axis=0
    )
    kv_prev = shifted(kv_chip, "blk", 1)
    kv_next = shifted(kv_chip, "blk", -1)

    padded_segs = jnp.concatenate(
        [jnp.full((block_len,), -2, jnp.int32), segment_ids, jnp.full((block_len,), -2, jnp.int32)]
    )

    def segs_at(begin, length):
        return lax.dynamic_slice_in_dim(padded_segs, begin + block_len, length)

    kv_sets = [kv_chip, from_right, from_left, relay, kv_prev, kv_next]
    seg_sets = [
        segs_at(b * block_len + xi * chunk, chunk),
        segs_at(b * block_len + ((xi + 1) % chips) * chunk, chunk),
        segs_at(b * block_len + ((xi + chips - 1) % chips) * chunk, chunk),
        segs_at(b * block_len + ((xi + 2) % chips) * chunk, chunk),
        segs_at((b - 1) * block_len + xi * chunk, chunk),
        segs_at((b + 1) * block_len + xi * chunk, chunk),
    ]
    half = chips // 2
    far = relay
    pairs = []
    for bb in range(group_count):
        for xx in range(chips):
            for cc in range(cores):
                to = bb + 1 if xx < half else bb - 1
                if 0 <= to < group_count:
                    pairs.append(((bb * chips + xx) * cores + cc, (to * chips + xx) * cores + cc))
    kv_sets.append(lax.ppermute(far, ALL, pairs))
    seg_sets.append(
        segs_at(
            jnp.where(
                xi < half,
                (b - 1) * block_len + (xi + half) * chunk,
                (b + 1) * block_len + (xi - half) * chunk,
            ),
            chunk,
        )
    )
    for s in (1, chips - 1):
        send = jnp.where(xi >= s, kv_prev, kv_next)
        kv_sets.append(cyclic(send, "x", -s))
        src = xi + s
        begin = jnp.where(
            src < chips,
            (b - 1) * block_len + src * chunk,
            (b + 1) * block_len + (src - chips) * chunk,
        )
        seg_sets.append(segs_at(begin, chunk))

    query_segs = lax.dynamic_slice_in_dim(segment_ids, chip_begin, chunk)
    query_heads = q_chip.reshape(chunk, slot_heads, HEAD)
    live = query_segs[:, None] >= 0
    blocks = []
    for kv, key_segs in zip(kv_sets, seg_sets):
        allowed = (query_segs[:, None] == key_segs[None, :]) & live
        key_heads = kv[:, :slot].reshape(kv.shape[0], slot_heads, HEAD)
        value_heads = kv[:, slot:].reshape(kv.shape[0], slot_heads, HEAD)
        scores = jnp.where(allowed[None], key_scores(query_heads, key_heads), masked_score)
        blocks.append((scores, allowed, value_heads))
    row_top = blocks[0][0].max(axis=2, keepdims=True)
    for scores, _, _ in blocks[1:]:
        row_top = jnp.maximum(row_top, scores.max(axis=2, keepdims=True))
    row_total = None
    mixed_out = None
    for scores, allowed, value_heads in blocks:
        exp_terms = jnp.where(allowed[None], jnp.exp(scores - row_top), 0.0)
        total = jnp.sum(exp_terms, axis=2)
        part = jnp.einsum(
            "hrk,khd->rhd", exp_terms.astype(jnp.bfloat16), value_heads,
            preferred_element_type=jnp.float32,
        )
        row_total = total if row_total is None else row_total + total
        mixed_out = part if mixed_out is None else mixed_out + part
    row_total = jnp.maximum(row_total, 1.0)
    mixed = (mixed_out / row_total.T[:, :, None]).reshape(chunk, slot).astype(jnp.bfloat16)

    mine = lax.dynamic_slice_in_dim(mixed, c * row_count, row_count)
    theirs = lax.dynamic_slice_in_dim(mixed, (1 - c) * row_count, row_count)
    back = cyclic(theirs, "core", 1)
    overlap = 2 * slot - width
    attended = jnp.where(
        first,
        jnp.concatenate([mine, back[:, overlap:]], axis=1),
        jnp.concatenate([back[:, : width - slot], mine], axis=1),
    )

    merged = attended.reshape(row_count // 4, 4 * width)
    piece = merged.shape[0]
    m_right = cyclic(merged, "x", -1)
    m_left = cyclic(merged, "x", 1)
    m_far = jnp.concatenate(
        [cyclic(m_right[: piece // 2], "x", -1), cyclic(m_left[piece // 2 :], "x", 1)], axis=0
    )
    mine4 = jnp.stack([merged, m_right, m_left, m_far])
    sib4 = cyclic(mine4, "core", 1)
    gathered = jnp.zeros((piece * chips * cores, merged.shape[1]), merged.dtype)
    for k, dx in enumerate((0, 1, chips - 1, 2)):
        at = (xi + dx) % chips
        gathered = lax.dynamic_update_slice_in_dim(gathered, mine4[k], (at * cores + c) * piece, 0)
        gathered = lax.dynamic_update_slice_in_dim(gathered, sib4[k], (at * cores + 1 - c) * piece, 0)
    projected = jnp.dot(gathered, proj_weight, preferred_element_type=jnp.float32)
    own_begin = b * block_len
    row_segs = lax.dynamic_slice_in_dim(segment_ids, own_begin, block_len)[::4]
    member = row_segs[:, None] == jnp.arange(group_count, dtype=jnp.int32)[None, :]
    squares = jnp.sum(projected * projected, axis=1)
    seg_sums = jnp.sum(jnp.where(member, squares[:, None], 0.0), axis=0)
    row_peak = jnp.max(jnp.where(member, jnp.max(projected, axis=1)[:, None], masked_score), axis=0)
    all_segs = segment_ids[::4]
    all_member = all_segs[:, None] == jnp.arange(group_count, dtype=jnp.int32)[None, :]
    seg_counts = jnp.sum(all_member.astype(jnp.float32), axis=0) * (
        projected.shape[1] * chips * cores
    )
    seg_sums, row_peak = butterfly(seg_sums, row_peak)
    seg_scale = lax.rsqrt(seg_sums / seg_counts + epsilon)
    row_scale = jnp.sum(jnp.where(member, seg_scale[None, :], 0.0), axis=1)
    normed = (projected * row_scale[:, None]).astype(jnp.bfloat16)
    return (normed, row_peak * seg_scale)


def solution(mesh):
    blk, tp = mesh.devices.shape
    cores = 2
    chip_mesh = Mesh(mesh.devices.reshape(blk, tp // cores, cores), ALL)
    rows = P(ALL, None)
    in_specs = (rows, rows, rows, P(), P(None, ("x", "core")))
    out_specs = (P("blk", ("x", "core")), P())
    return jax.shard_map(
        per_device, mesh=chip_mesh, in_specs=in_specs, out_specs=out_specs, check_vma=False
    )
```

```python
import jax
import jax.numpy as jnp
from jax import lax
from jax.sharding import Mesh
from jax.sharding import PartitionSpec as P

HEAD = 128


masked_score = -1e30
epsilon = 1e-06

ALL = ("blk", "x", "core")


def key_scores(query_heads, key_heads):
    return jnp.einsum(
        "rhd,khd->hrk", query_heads, key_heads, preferred_element_type=jnp.float32
    ) * HEAD ** (-0.5)


def finish(scores, allowed, value_heads):
    scores = jnp.where(allowed[None], scores, masked_score)
    row_top = jnp.max(scores, axis=2, keepdims=True)
    exp_terms = jnp.where(allowed[None], jnp.exp(scores - row_top), 0.0)
    row_total = jnp.maximum(jnp.sum(exp_terms, axis=2), 1.0)
    weights = exp_terms.astype(jnp.bfloat16)
    mixed_out = jnp.einsum("hrk,khd->rhd", weights, value_heads, preferred_element_type=jnp.float32)
    return mixed_out / row_total.T[:, :, None]


def shifted(x, axis, by):
    n = lax.axis_size(axis)
    return lax.ppermute(x, axis, [(i, i + by) for i in range(n) if 0 <= i + by < n])


def cyclic(x, axis, by):
    n = lax.axis_size(axis)
    return lax.ppermute(x, axis, [(i, (i + by) % n) for i in range(n)])


def butterfly(sums, peaks):
    n = 1
    for name in ALL:
        n *= lax.axis_size(name)
    bit = 1
    while bit < n:
        perm = [(i, i ^ bit) for i in range(n)]
        other = lax.ppermute(jnp.stack([sums, peaks]), ALL, perm)
        sums = sums + other[0]
        peaks = jnp.maximum(peaks, other[1])
        bit *= 2
    return sums, peaks


def per_device(queries, keys, values, segment_ids, proj_weight):
    group_count = lax.axis_size("blk")
    chips = lax.axis_size("x")
    cores = lax.axis_size("core")
    b = lax.axis_index("blk")
    xi = lax.axis_index("x")
    c = lax.axis_index("core")
    row_count, width = queries.shape
    heads_count = width // HEAD
    slot_heads = -(-heads_count // cores)
    slot = slot_heads * HEAD
    block_len = segment_ids.shape[0] // group_count
    chunk = row_count * cores
    chip_begin = b * block_len + xi * chunk

    my_col = c * (width - slot)
    sib_col = (1 - c) * (width - slot)

    def cols(a, at):
        return lax.dynamic_slice_in_dim(a, at, slot, axis=1)

    own = jnp.concatenate([cols(queries, my_col), cols(keys, my_col), cols(values, my_col)], axis=1)
    give = jnp.concatenate([cols(queries, sib_col), cols(keys, sib_col), cols(values, sib_col)], axis=1)
    got = cyclic(give, "core", 1)
    first = c == 0
    chip_rows = jnp.concatenate(
        [jnp.where(first, own, got), jnp.where(first, got, own)], axis=0
    )
    q_chip = chip_rows[:, :slot]
    kv_chip = chip_rows[:, slot:]

    right_a = cyclic(kv_chip[:row_count], "x", -1)
    left_b = cyclic(kv_chip[row_count:], "x", 1)
    right_a, left_b, rest = lax.optimization_barrier((right_a, left_b, kv_chip))
    right_b = cyclic(rest[row_count:], "x", -1)
    left_a = cyclic(rest[:row_count], "x", 1)
    from_right = jnp.concatenate([right_a, right_b], axis=0)
    from_left = jnp.concatenate([left_a, left_b], axis=0)
    relay = jnp.concatenate([cyclic(right_a, "x", -1), cyclic(left_b, "x", 1)], axis=0)
    kv_prev = shifted(kv_chip, "blk", 1)
    kv_next = shifted(kv_chip, "blk", -1)

    padded_segs = jnp.concatenate(
        [jnp.full((block_len,), -2, jnp.int32), segment_ids, jnp.full((block_len,), -2, jnp.int32)]
    )

    def segs_at(begin, length):
        return lax.dynamic_slice_in_dim(padded_segs, begin + block_len, length)

    kv_sets = [kv_chip, from_right, from_left, relay, kv_prev, kv_next]
    seg_sets = [
        segs_at(b * block_len + xi * chunk, chunk),
        segs_at(b * block_len + ((xi + 1) % chips) * chunk, chunk),
        segs_at(b * block_len + ((xi + chips - 1) % chips) * chunk, chunk),
        segs_at(b * block_len + ((xi + 2) % chips) * chunk, chunk),
        segs_at((b - 1) * block_len + xi * chunk, chunk),
        segs_at((b + 1) * block_len + xi * chunk, chunk),
    ]
    half = chips // 2
    far = relay
    pairs = []
    for bb in range(group_count):
        for xx in range(chips):
            for cc in range(cores):
                to = bb + 1 if xx < half else bb - 1
                if 0 <= to < group_count:
                    pairs.append(((bb * chips + xx) * cores + cc, (to * chips + xx) * cores + cc))
    kv_sets.append(lax.ppermute(far, ALL, pairs))
    seg_sets.append(
        segs_at(
            jnp.where(
                xi < half,
                (b - 1) * block_len + (xi + half) * chunk,
                (b + 1) * block_len + (xi - half) * chunk,
            ),
            chunk,
        )
    )
    for s in (1, chips - 1):
        send = jnp.where(xi >= s, kv_prev, kv_next)
        kv_sets.append(cyclic(send, "x", -s))
        src = xi + s
        begin = jnp.where(
            src < chips,
            (b - 1) * block_len + src * chunk,
            (b + 1) * block_len + (src - chips) * chunk,
        )
        seg_sets.append(segs_at(begin, chunk))

    query_segs = lax.dynamic_slice_in_dim(segment_ids, chip_begin, chunk)
    query_heads = q_chip.reshape(chunk, slot_heads, HEAD)
    live = query_segs[:, None] >= 0
    blocks = []
    for kv, key_segs in zip(kv_sets, seg_sets):
        allowed = (query_segs[:, None] == key_segs[None, :]) & live
        key_heads = kv[:, :slot].reshape(kv.shape[0], slot_heads, HEAD)
        value_heads = kv[:, slot:].reshape(kv.shape[0], slot_heads, HEAD)
        scores = jnp.where(allowed[None], key_scores(query_heads, key_heads), masked_score)
        blocks.append((scores, allowed, value_heads))
    row_top = blocks[0][0].max(axis=2, keepdims=True)
    for scores, _, _ in blocks[1:]:
        row_top = jnp.maximum(row_top, scores.max(axis=2, keepdims=True))
    row_total = None
    mixed_out = None
    for scores, allowed, value_heads in blocks:
        exp_terms = jnp.where(allowed[None], jnp.exp(scores - row_top), 0.0)
        total = jnp.sum(exp_terms, axis=2)
        part = jnp.einsum(
            "hrk,khd->rhd", exp_terms.astype(jnp.bfloat16), value_heads,
            preferred_element_type=jnp.float32,
        )
        row_total = total if row_total is None else row_total + total
        mixed_out = part if mixed_out is None else mixed_out + part
    row_total = jnp.maximum(row_total, 1.0)
    mixed = (mixed_out / row_total.T[:, :, None]).reshape(chunk, slot).astype(jnp.bfloat16)

    mine = lax.dynamic_slice_in_dim(mixed, c * row_count, row_count)
    theirs = lax.dynamic_slice_in_dim(mixed, (1 - c) * row_count, row_count)
    back = cyclic(theirs, "core", 1)
    overlap = 2 * slot - width
    attended = jnp.where(
        first,
        jnp.concatenate([mine, back[:, overlap:]], axis=1),
        jnp.concatenate([back[:, : width - slot], mine], axis=1),
    )

    merged = attended.reshape(row_count // 4, 4 * width)
    piece = merged.shape[0]
    m_right = cyclic(merged, "x", -1)
    m_left = cyclic(merged, "x", 1)
    m_far = jnp.concatenate(
        [cyclic(m_right[: piece // 2], "x", -1), cyclic(m_left[piece // 2 :], "x", 1)], axis=0
    )
    mine4 = jnp.stack([merged, m_right, m_left, m_far])
    sib4 = cyclic(mine4, "core", 1)
    gathered = jnp.zeros((piece * chips * cores, merged.shape[1]), merged.dtype)
    for k, dx in enumerate((0, 1, chips - 1, 2)):
        at = (xi + dx) % chips
        gathered = lax.dynamic_update_slice_in_dim(gathered, mine4[k], (at * cores + c) * piece, 0)
        gathered = lax.dynamic_update_slice_in_dim(gathered, sib4[k], (at * cores + 1 - c) * piece, 0)
    projected = jnp.dot(gathered, proj_weight, preferred_element_type=jnp.float32)
    own_begin = b * block_len
    row_segs = lax.dynamic_slice_in_dim(segment_ids, own_begin, block_len)[::4]
    member = row_segs[:, None] == jnp.arange(group_count, dtype=jnp.int32)[None, :]
    squares = jnp.sum(projected * projected, axis=1)
    seg_sums = jnp.sum(jnp.where(member, squares[:, None], 0.0), axis=0)
    row_peak = jnp.max(jnp.where(member, jnp.max(projected, axis=1)[:, None], masked_score), axis=0)
    all_segs = segment_ids[::4]
    all_member = all_segs[:, None] == jnp.arange(group_count, dtype=jnp.int32)[None, :]
    seg_counts = jnp.sum(all_member.astype(jnp.float32), axis=0) * (
        projected.shape[1] * chips * cores
    )
    seg_sums, row_peak = butterfly(seg_sums, row_peak)
    seg_scale = lax.rsqrt(seg_sums / seg_counts + epsilon)
    row_scale = jnp.sum(jnp.where(member, seg_scale[None, :], 0.0), axis=1)
    normed = (projected * row_scale[:, None]).astype(jnp.bfloat16)
    return (normed, row_peak * seg_scale)


def solution(mesh):
    blk, tp = mesh.devices.shape
    cores = 2
    chip_mesh = Mesh(mesh.devices.reshape(blk, tp // cores, cores), ALL)
    rows = P(ALL, None)
    in_specs = (rows, rows, rows, P(), P(None, ("x", "core")))
    out_specs = (P("blk", ("x", "core")), P())
    return jax.shard_map(
        per_device, mesh=chip_mesh, in_specs=in_specs, out_specs=out_specs, check_vma=False
    )
```

```python
import jax
import jax.numpy as jnp
from jax import lax
from jax.sharding import Mesh
from jax.sharding import PartitionSpec as P

HEAD = 128


masked_score = -1e30
epsilon = 1e-06

ALL = ("blk", "x", "core")


def key_scores(query_heads, key_heads):
    return jnp.einsum(
        "rhd,khd->hrk", query_heads, key_heads, preferred_element_type=jnp.float32
    ) * HEAD ** (-0.5)


def finish(scores, allowed, value_heads):
    scores = jnp.where(allowed[None], scores, masked_score)
    row_top = jnp.max(scores, axis=2, keepdims=True)
    exp_terms = jnp.where(allowed[None], jnp.exp(scores - row_top), 0.0)
    row_total = jnp.maximum(jnp.sum(exp_terms, axis=2), 1.0)
    weights = exp_terms.astype(jnp.bfloat16)
    mixed_out = jnp.einsum("hrk,khd->rhd", weights, value_heads, preferred_element_type=jnp.float32)
    return mixed_out / row_total.T[:, :, None]


def shifted(x, axis, by):
    n = lax.axis_size(axis)
    return lax.ppermute(x, axis, [(i, i + by) for i in range(n) if 0 <= i + by < n])


def cyclic(x, axis, by):
    n = lax.axis_size(axis)
    return lax.ppermute(x, axis, [(i, (i + by) % n) for i in range(n)])


def butterfly(sums, peaks):
    n = 1
    for name in ALL:
        n *= lax.axis_size(name)
    bit = 1
    while bit < n:
        perm = [(i, i ^ bit) for i in range(n)]
        other = lax.ppermute(jnp.stack([sums, peaks]), ALL, perm)
        sums = sums + other[0]
        peaks = jnp.maximum(peaks, other[1])
        bit *= 2
    return sums, peaks


def per_device(queries, keys, values, segment_ids, proj_weight):
    group_count = lax.axis_size("blk")
    chips = lax.axis_size("x")
    cores = lax.axis_size("core")
    b = lax.axis_index("blk")
    xi = lax.axis_index("x")
    c = lax.axis_index("core")
    row_count, width = queries.shape
    heads_count = width // HEAD
    slot_heads = -(-heads_count // cores)
    slot = slot_heads * HEAD
    block_len = segment_ids.shape[0] // group_count
    chunk = row_count * cores
    chip_begin = b * block_len + xi * chunk

    my_col = c * (width - slot)
    sib_col = (1 - c) * (width - slot)

    def cols(a, at):
        return lax.dynamic_slice_in_dim(a, at, slot, axis=1)

    own = jnp.concatenate([cols(queries, my_col), cols(keys, my_col), cols(values, my_col)], axis=1)
    give = jnp.concatenate([cols(queries, sib_col), cols(keys, sib_col), cols(values, sib_col)], axis=1)
    got = cyclic(give, "core", 1)
    first = c == 0
    chip_rows = jnp.concatenate(
        [jnp.where(first, own, got), jnp.where(first, got, own)], axis=0
    )
    q_chip = chip_rows[:, :slot]
    kv_chip = chip_rows[:, slot:]

    right_a = cyclic(kv_chip[:row_count], "x", -1)
    left_b = cyclic(kv_chip[row_count:], "x", 1)
    right_a, left_b, rest = lax.optimization_barrier((right_a, left_b, kv_chip))
    right_b = cyclic(rest[row_count:], "x", -1)
    left_a = cyclic(rest[:row_count], "x", 1)
    from_right = jnp.concatenate([right_a, right_b], axis=0)
    from_left = jnp.concatenate([left_a, left_b], axis=0)
    relay = jnp.concatenate([cyclic(right_a, "x", -1), cyclic(left_b, "x", 1)], axis=0)
    kv_prev = shifted(kv_chip, "blk", 1)
    kv_next = shifted(kv_chip, "blk", -1)

    padded_segs = jnp.concatenate(
        [jnp.full((block_len,), -2, jnp.int32), segment_ids, jnp.full((block_len,), -2, jnp.int32)]
    )

    def segs_at(begin, length):
        return lax.dynamic_slice_in_dim(padded_segs, begin + block_len, length)

    kv_sets = [kv_chip, from_right, from_left, relay, kv_prev, kv_next]
    seg_sets = [
        segs_at(b * block_len + xi * chunk, chunk),
        segs_at(b * block_len + ((xi + 1) % chips) * chunk, chunk),
        segs_at(b * block_len + ((xi + chips - 1) % chips) * chunk, chunk),
        segs_at(b * block_len + ((xi + 2) % chips) * chunk, chunk),
        segs_at((b - 1) * block_len + xi * chunk, chunk),
        segs_at((b + 1) * block_len + xi * chunk, chunk),
    ]
    half = chips // 2
    far = relay
    pairs = []
    for bb in range(group_count):
        for xx in range(chips):
            for cc in range(cores):
                to = bb + 1 if xx < half else bb - 1
                if 0 <= to < group_count:
                    pairs.append(((bb * chips + xx) * cores + cc, (to * chips + xx) * cores + cc))
    kv_sets.append(lax.ppermute(far, ALL, pairs))
    seg_sets.append(
        segs_at(
            jnp.where(
                xi < half,
                (b - 1) * block_len + (xi + half) * chunk,
                (b + 1) * block_len + (xi - half) * chunk,
            ),
            chunk,
        )
    )
    for s in (1, chips - 1):
        send = jnp.where(xi >= s, kv_prev, kv_next)
        kv_sets.append(cyclic(send, "x", -s))
        src = xi + s
        begin = jnp.where(
            src < chips,
            (b - 1) * block_len + src * chunk,
            (b + 1) * block_len + (src - chips) * chunk,
        )
        seg_sets.append(segs_at(begin, chunk))

    query_segs = lax.dynamic_slice_in_dim(segment_ids, chip_begin, chunk)
    query_heads = q_chip.reshape(chunk, slot_heads, HEAD)
    live = query_segs[:, None] >= 0
    blocks = []
    for kv, key_segs in zip(kv_sets, seg_sets):
        allowed = (query_segs[:, None] == key_segs[None, :]) & live
        key_heads = kv[:, :slot].reshape(kv.shape[0], slot_heads, HEAD)
        value_heads = kv[:, slot:].reshape(kv.shape[0], slot_heads, HEAD)
        scores = jnp.where(allowed[None], key_scores(query_heads, key_heads), masked_score)
        blocks.append((scores, allowed, value_heads))
    def accumulate(group, row_top):
        row_total = None
        mixed_out = None
        for scores, allowed, value_heads in group:
            exp_terms = jnp.where(allowed[None], jnp.exp(scores - row_top), 0.0)
            total = jnp.sum(exp_terms, axis=2)
            part = jnp.einsum(
                "hrk,khd->rhd", exp_terms.astype(jnp.bfloat16), value_heads,
                preferred_element_type=jnp.float32,
            )
            row_total = total if row_total is None else row_total + total
            mixed_out = part if mixed_out is None else mixed_out + part
        return row_total, mixed_out

    def group_top(group):
        top = group[0][0].max(axis=2, keepdims=True)
        for scores, _, _ in group[1:]:
            top = jnp.maximum(top, scores.max(axis=2, keepdims=True))
        return top

    early, late = blocks[:6], blocks[6:]
    early_top = group_top(early)
    early_total, early_out = accumulate(early, early_top)
    row_top = jnp.maximum(early_top, group_top(late))
    late_total, late_out = accumulate(late, row_top)
    rescale = jnp.exp(early_top - row_top)
    row_total = jnp.maximum(early_total * rescale[:, :, 0] + late_total, 1.0)
    mixed_out = early_out * rescale[:, :, 0].T[:, :, None] + late_out
    mixed = (mixed_out / row_total.T[:, :, None]).reshape(chunk, slot).astype(jnp.bfloat16)

    mine = lax.dynamic_slice_in_dim(mixed, c * row_count, row_count)
    theirs = lax.dynamic_slice_in_dim(mixed, (1 - c) * row_count, row_count)
    back = cyclic(theirs, "core", 1)
    overlap = 2 * slot - width
    attended = jnp.where(
        first,
        jnp.concatenate([mine, back[:, overlap:]], axis=1),
        jnp.concatenate([back[:, : width - slot], mine], axis=1),
    )

    merged = attended.reshape(row_count // 4, 4 * width)
    piece = merged.shape[0]
    m_right = cyclic(merged, "x", -1)
    m_left = cyclic(merged, "x", 1)
    m_far = jnp.concatenate(
        [cyclic(m_right[: piece // 2], "x", -1), cyclic(m_left[piece // 2 :], "x", 1)], axis=0
    )
    mine4 = jnp.stack([merged, m_right, m_left, m_far])
    sib4 = cyclic(mine4, "core", 1)
    gathered = jnp.zeros((piece * chips * cores, merged.shape[1]), merged.dtype)
    for k, dx in enumerate((0, 1, chips - 1, 2)):
        at = (xi + dx) % chips
        gathered = lax.dynamic_update_slice_in_dim(gathered, mine4[k], (at * cores + c) * piece, 0)
        gathered = lax.dynamic_update_slice_in_dim(gathered, sib4[k], (at * cores + 1 - c) * piece, 0)
    projected = jnp.dot(gathered, proj_weight, preferred_element_type=jnp.float32)
    own_begin = b * block_len
    row_segs = lax.dynamic_slice_in_dim(segment_ids, own_begin, block_len)[::4]
    member = row_segs[:, None] == jnp.arange(group_count, dtype=jnp.int32)[None, :]
    squares = jnp.sum(projected * projected, axis=1)
    seg_sums = jnp.sum(jnp.where(member, squares[:, None], 0.0), axis=0)
    row_peak = jnp.max(jnp.where(member, jnp.max(projected, axis=1)[:, None], masked_score), axis=0)
    all_segs = segment_ids[::4]
    all_member = all_segs[:, None] == jnp.arange(group_count, dtype=jnp.int32)[None, :]
    seg_counts = jnp.sum(all_member.astype(jnp.float32), axis=0) * (
        projected.shape[1] * chips * cores
    )
    seg_sums, row_peak = butterfly(seg_sums, row_peak)
    seg_scale = lax.rsqrt(seg_sums / seg_counts + epsilon)
    row_scale = jnp.sum(jnp.where(member, seg_scale[None, :], 0.0), axis=1)
    normed = (projected * row_scale[:, None]).astype(jnp.bfloat16)
    return (normed, row_peak * seg_scale)


def solution(mesh):
    blk, tp = mesh.devices.shape
    cores = 2
    chip_mesh = Mesh(mesh.devices.reshape(blk, tp // cores, cores), ALL)
    rows = P(ALL, None)
    in_specs = (rows, rows, rows, P(), P(None, ("x", "core")))
    out_specs = (P("blk", ("x", "core")), P())
    return jax.shard_map(
        per_device, mesh=chip_mesh, in_specs=in_specs, out_specs=out_specs, check_vma=False
    )
```

```python
import jax
import jax.numpy as jnp
from jax import lax
from jax.sharding import Mesh
from jax.sharding import PartitionSpec as P

HEAD = 128


masked_score = -1e30
epsilon = 1e-06

ALL = ("blk", "x", "core")


def key_scores(query_heads, key_heads):
    return jnp.einsum(
        "rhd,khd->hrk", query_heads, key_heads, preferred_element_type=jnp.float32
    ) * HEAD ** (-0.5)


def finish(scores, allowed, value_heads):
    scores = jnp.where(allowed[None], scores, masked_score)
    row_top = jnp.max(scores, axis=2, keepdims=True)
    exp_terms = jnp.where(allowed[None], jnp.exp(scores - row_top), 0.0)
    row_total = jnp.maximum(jnp.sum(exp_terms, axis=2), 1.0)
    weights = exp_terms.astype(jnp.bfloat16)
    mixed_out = jnp.einsum("hrk,khd->rhd", weights, value_heads, preferred_element_type=jnp.float32)
    return mixed_out / row_total.T[:, :, None]


def shifted(x, axis, by):
    n = lax.axis_size(axis)
    return lax.ppermute(x, axis, [(i, i + by) for i in range(n) if 0 <= i + by < n])


def cyclic(x, axis, by):
    n = lax.axis_size(axis)
    return lax.ppermute(x, axis, [(i, (i + by) % n) for i in range(n)])


def butterfly(sums, peaks):
    n = 1
    for name in ALL:
        n *= lax.axis_size(name)
    bit = 1
    while bit < n:
        perm = [(i, i ^ bit) for i in range(n)]
        other = lax.ppermute(jnp.stack([sums, peaks]), ALL, perm)
        sums = sums + other[0]
        peaks = jnp.maximum(peaks, other[1])
        bit *= 2
    return sums, peaks


def per_device(queries, keys, values, segment_ids, proj_weight):
    group_count = lax.axis_size("blk")
    chips = lax.axis_size("x")
    cores = lax.axis_size("core")
    b = lax.axis_index("blk")
    xi = lax.axis_index("x")
    c = lax.axis_index("core")
    row_count, width = queries.shape
    heads_count = width // HEAD
    slot_heads = -(-heads_count // cores)
    slot = slot_heads * HEAD
    block_len = segment_ids.shape[0] // group_count
    chunk = row_count * cores
    chip_begin = b * block_len + xi * chunk

    my_col = c * (width - slot)
    sib_col = (1 - c) * (width - slot)

    def cols(a, at):
        return lax.dynamic_slice_in_dim(a, at, slot, axis=1)

    own = jnp.concatenate([cols(queries, my_col), cols(keys, my_col), cols(values, my_col)], axis=1)
    give = jnp.concatenate([cols(queries, sib_col), cols(keys, sib_col), cols(values, sib_col)], axis=1)
    got = cyclic(give, "core", 1)
    first = c == 0
    chip_rows = jnp.concatenate(
        [jnp.where(first, own, got), jnp.where(first, got, own)], axis=0
    )
    q_chip = chip_rows[:, :slot]
    kv_chip = chip_rows[:, slot:]

    right_a = cyclic(kv_chip[:row_count], "x", -1)
    left_b = cyclic(kv_chip[row_count:], "x", 1)
    right_a, left_b, rest = lax.optimization_barrier((right_a, left_b, kv_chip))
    right_b = cyclic(rest[row_count:], "x", -1)
    left_a = cyclic(rest[:row_count], "x", 1)
    from_right = jnp.concatenate([right_a, right_b], axis=0)
    from_left = jnp.concatenate([left_a, left_b], axis=0)
    relay = jnp.concatenate([cyclic(right_a, "x", -1), cyclic(left_b, "x", 1)], axis=0)
    kv_prev = shifted(kv_chip, "blk", 1)
    kv_next = shifted(kv_chip, "blk", -1)

    padded_segs = jnp.concatenate(
        [jnp.full((block_len,), -2, jnp.int32), segment_ids, jnp.full((block_len,), -2, jnp.int32)]
    )

    def segs_at(begin, length):
        return lax.dynamic_slice_in_dim(padded_segs, begin + block_len, length)

    kv_sets = [kv_chip, from_right, from_left, relay, kv_prev, kv_next]
    seg_sets = [
        segs_at(b * block_len + xi * chunk, chunk),
        segs_at(b * block_len + ((xi + 1) % chips) * chunk, chunk),
        segs_at(b * block_len + ((xi + chips - 1) % chips) * chunk, chunk),
        segs_at(b * block_len + ((xi + 2) % chips) * chunk, chunk),
        segs_at((b - 1) * block_len + xi * chunk, chunk),
        segs_at((b + 1) * block_len + xi * chunk, chunk),
    ]
    half = chips // 2
    far = relay
    pairs = []
    for bb in range(group_count):
        for xx in range(chips):
            for cc in range(cores):
                to = bb + 1 if xx < half else bb - 1
                if 0 <= to < group_count:
                    pairs.append(((bb * chips + xx) * cores + cc, (to * chips + xx) * cores + cc))
    kv_sets.append(lax.ppermute(far, ALL, pairs))
    seg_sets.append(
        segs_at(
            jnp.where(
                xi < half,
                (b - 1) * block_len + (xi + half) * chunk,
                (b + 1) * block_len + (xi - half) * chunk,
            ),
            chunk,
        )
    )
    for s in (1, chips - 1):
        send = jnp.where(xi >= s, kv_prev, kv_next)
        kv_sets.append(cyclic(send, "x", -s))
        src = xi + s
        begin = jnp.where(
            src < chips,
            (b - 1) * block_len + src * chunk,
            (b + 1) * block_len + (src - chips) * chunk,
        )
        seg_sets.append(segs_at(begin, chunk))

    query_segs = lax.dynamic_slice_in_dim(segment_ids, chip_begin, chunk)
    query_heads = q_chip.reshape(chunk, slot_heads, HEAD)
    live = query_segs[:, None] >= 0
    blocks = []
    for kv, key_segs in zip(kv_sets, seg_sets):
        allowed = (query_segs[:, None] == key_segs[None, :]) & live
        key_heads = kv[:, :slot].reshape(kv.shape[0], slot_heads, HEAD)
        value_heads = kv[:, slot:].reshape(kv.shape[0], slot_heads, HEAD)
        scores = jnp.where(allowed[None], key_scores(query_heads, key_heads), masked_score)
        blocks.append((scores, allowed, value_heads))
    row_top = blocks[0][0].max(axis=2, keepdims=True)
    for scores, _, _ in blocks[1:]:
        row_top = jnp.maximum(row_top, scores.max(axis=2, keepdims=True))
    row_total = None
    mixed_out = None
    for scores, allowed, value_heads in blocks:
        exp_terms = jnp.where(allowed[None], jnp.exp(scores - row_top), 0.0)
        total = jnp.sum(exp_terms, axis=2)
        part = jnp.einsum(
            "hrk,khd->rhd", exp_terms.astype(jnp.bfloat16), value_heads,
            preferred_element_type=jnp.float32,
        )
        row_total = total if row_total is None else row_total + total
        mixed_out = part if mixed_out is None else mixed_out + part
    row_total = jnp.maximum(row_total, 1.0)
    mixed = (mixed_out / row_total.T[:, :, None]).reshape(chunk, slot).astype(jnp.bfloat16)

    mine = lax.dynamic_slice_in_dim(mixed, c * row_count, row_count)
    theirs = lax.dynamic_slice_in_dim(mixed, (1 - c) * row_count, row_count)
    back = cyclic(theirs, "core", 1)
    overlap = 2 * slot - width
    attended = jnp.where(
        first,
        jnp.concatenate([mine, back[:, overlap:]], axis=1),
        jnp.concatenate([back[:, : width - slot], mine], axis=1),
    )

    merged = attended.reshape(row_count // 4, 4 * width)
    piece = merged.shape[0]
    sib_own = cyclic(merged, "core", 1)
    m_right_a = cyclic(merged[: piece // 2], "x", -1)
    m_left_b = cyclic(merged[piece // 2 :], "x", 1)
    m_right_a, m_left_b, m_rest = lax.optimization_barrier((m_right_a, m_left_b, merged))
    m_right = jnp.concatenate([m_right_a, cyclic(m_rest[piece // 2 :], "x", -1)], axis=0)
    m_left = jnp.concatenate([cyclic(m_rest[: piece // 2], "x", 1), m_left_b], axis=0)
    m_far = jnp.concatenate([cyclic(m_right_a, "x", -1), cyclic(m_left_b, "x", 1)], axis=0)
    mine4 = jnp.stack([merged, m_right, m_left, m_far])
    sib3 = cyclic(mine4[1:], "core", 1)
    sib4 = jnp.concatenate([sib_own[None], sib3], axis=0)
    gathered = jnp.zeros((piece * chips * cores, merged.shape[1]), merged.dtype)
    for k, dx in enumerate((0, 1, chips - 1, 2)):
        at = (xi + dx) % chips
        gathered = lax.dynamic_update_slice_in_dim(gathered, mine4[k], (at * cores + c) * piece, 0)
        gathered = lax.dynamic_update_slice_in_dim(gathered, sib4[k], (at * cores + 1 - c) * piece, 0)
    projected = jnp.dot(gathered, proj_weight, preferred_element_type=jnp.float32)
    own_begin = b * block_len
    row_segs = lax.dynamic_slice_in_dim(segment_ids, own_begin, block_len)[::4]
    member = row_segs[:, None] == jnp.arange(group_count, dtype=jnp.int32)[None, :]
    squares = jnp.sum(projected * projected, axis=1)
    seg_sums = jnp.sum(jnp.where(member, squares[:, None], 0.0), axis=0)
    row_peak = jnp.max(jnp.where(member, jnp.max(projected, axis=1)[:, None], masked_score), axis=0)
    all_segs = segment_ids[::4]
    all_member = all_segs[:, None] == jnp.arange(group_count, dtype=jnp.int32)[None, :]
    seg_counts = jnp.sum(all_member.astype(jnp.float32), axis=0) * (
        projected.shape[1] * chips * cores
    )
    seg_sums, row_peak = butterfly(seg_sums, row_peak)
    seg_scale = lax.rsqrt(seg_sums / seg_counts + epsilon)
    row_scale = jnp.sum(jnp.where(member, seg_scale[None, :], 0.0), axis=1)
    normed = (projected * row_scale[:, None]).astype(jnp.bfloat16)
    return (normed, row_peak * seg_scale)


def solution(mesh):
    blk, tp = mesh.devices.shape
    cores = 2
    chip_mesh = Mesh(mesh.devices.reshape(blk, tp // cores, cores), ALL)
    rows = P(ALL, None)
    in_specs = (rows, rows, rows, P(), P(None, ("x", "core")))
    out_specs = (P("blk", ("x", "core")), P())
    return jax.shard_map(
        per_device, mesh=chip_mesh, in_specs=in_specs, out_specs=out_specs, check_vma=False
    )
```

```python
import jax
import jax.numpy as jnp
from jax import lax
from jax.sharding import Mesh
from jax.sharding import PartitionSpec as P

HEAD = 128


masked_score = -1e30
epsilon = 1e-06

ALL = ("blk", "x", "core")


def key_scores(query_heads, key_heads):
    return jnp.einsum(
        "rhd,khd->hrk", query_heads, key_heads, preferred_element_type=jnp.float32
    ) * HEAD ** (-0.5)


def finish(scores, allowed, value_heads):
    scores = jnp.where(allowed[None], scores, masked_score)
    row_top = jnp.max(scores, axis=2, keepdims=True)
    exp_terms = jnp.where(allowed[None], jnp.exp(scores - row_top), 0.0)
    row_total = jnp.maximum(jnp.sum(exp_terms, axis=2), 1.0)
    weights = exp_terms.astype(jnp.bfloat16)
    mixed_out = jnp.einsum("hrk,khd->rhd", weights, value_heads, preferred_element_type=jnp.float32)
    return mixed_out / row_total.T[:, :, None]


def shifted(x, axis, by):
    n = lax.axis_size(axis)
    return lax.ppermute(x, axis, [(i, i + by) for i in range(n) if 0 <= i + by < n])


def cyclic(x, axis, by):
    n = lax.axis_size(axis)
    return lax.ppermute(x, axis, [(i, (i + by) % n) for i in range(n)])


def butterfly(sums, peaks):
    n = 1
    for name in ALL:
        n *= lax.axis_size(name)
    bit = 1
    while bit < n:
        perm = [(i, i ^ bit) for i in range(n)]
        other = lax.ppermute(jnp.stack([sums, peaks]), ALL, perm)
        sums = sums + other[0]
        peaks = jnp.maximum(peaks, other[1])
        bit *= 2
    return sums, peaks


def per_device(queries, keys, values, segment_ids, proj_weight):
    group_count = lax.axis_size("blk")
    chips = lax.axis_size("x")
    cores = lax.axis_size("core")
    b = lax.axis_index("blk")
    xi = lax.axis_index("x")
    c = lax.axis_index("core")
    row_count, width = queries.shape
    heads_count = width // HEAD
    slot_heads = -(-heads_count // cores)
    slot = slot_heads * HEAD
    block_len = segment_ids.shape[0] // group_count
    chunk = row_count * cores
    chip_begin = b * block_len + xi * chunk

    my_col = c * (width - slot)
    sib_col = (1 - c) * (width - slot)

    def cols(a, at):
        return lax.dynamic_slice_in_dim(a, at, slot, axis=1)

    own = jnp.concatenate([cols(queries, my_col), cols(keys, my_col), cols(values, my_col)], axis=1)
    give = jnp.concatenate([cols(queries, sib_col), cols(keys, sib_col), cols(values, sib_col)], axis=1)
    got = cyclic(give, "core", 1)
    first = c == 0
    chip_rows = jnp.concatenate(
        [jnp.where(first, own, got), jnp.where(first, got, own)], axis=0
    )
    q_chip = chip_rows[:, :slot]
    sib_weight = cyclic(proj_weight, "core", 1)
    chip_weight = jnp.where(
        first,
        jnp.concatenate([proj_weight, sib_weight], axis=1),
        jnp.concatenate([sib_weight, proj_weight], axis=1),
    )
    kv_chip = chip_rows[:, slot:]

    right_a = cyclic(kv_chip[:row_count], "x", -1)
    left_b = cyclic(kv_chip[row_count:], "x", 1)
    right_a, left_b, rest = lax.optimization_barrier((right_a, left_b, kv_chip))
    right_b = cyclic(rest[row_count:], "x", -1)
    left_a = cyclic(rest[:row_count], "x", 1)
    from_right = jnp.concatenate([right_a, right_b], axis=0)
    from_left = jnp.concatenate([left_a, left_b], axis=0)
    relay = jnp.concatenate([cyclic(right_a, "x", -1), cyclic(left_b, "x", 1)], axis=0)
    kv_prev = shifted(kv_chip, "blk", 1)
    kv_next = shifted(kv_chip, "blk", -1)

    padded_segs = jnp.concatenate(
        [jnp.full((block_len,), -2, jnp.int32), segment_ids, jnp.full((block_len,), -2, jnp.int32)]
    )

    def segs_at(begin, length):
        return lax.dynamic_slice_in_dim(padded_segs, begin + block_len, length)

    kv_sets = [kv_chip, from_right, from_left, relay, kv_prev, kv_next]
    seg_sets = [
        segs_at(b * block_len + xi * chunk, chunk),
        segs_at(b * block_len + ((xi + 1) % chips) * chunk, chunk),
        segs_at(b * block_len + ((xi + chips - 1) % chips) * chunk, chunk),
        segs_at(b * block_len + ((xi + 2) % chips) * chunk, chunk),
        segs_at((b - 1) * block_len + xi * chunk, chunk),
        segs_at((b + 1) * block_len + xi * chunk, chunk),
    ]
    half = chips // 2
    far = relay
    pairs = []
    for bb in range(group_count):
        for xx in range(chips):
            for cc in range(cores):
                to = bb + 1 if xx < half else bb - 1
                if 0 <= to < group_count:
                    pairs.append(((bb * chips + xx) * cores + cc, (to * chips + xx) * cores + cc))
    kv_sets.append(lax.ppermute(far, ALL, pairs))
    seg_sets.append(
        segs_at(
            jnp.where(
                xi < half,
                (b - 1) * block_len + (xi + half) * chunk,
                (b + 1) * block_len + (xi - half) * chunk,
            ),
            chunk,
        )
    )
    for s in (1, chips - 1):
        send = jnp.where(xi >= s, kv_prev, kv_next)
        kv_sets.append(cyclic(send, "x", -s))
        src = xi + s
        begin = jnp.where(
            src < chips,
            (b - 1) * block_len + src * chunk,
            (b + 1) * block_len + (src - chips) * chunk,
        )
        seg_sets.append(segs_at(begin, chunk))

    query_segs = lax.dynamic_slice_in_dim(segment_ids, chip_begin, chunk)
    query_heads = q_chip.reshape(chunk, slot_heads, HEAD)
    live = query_segs[:, None] >= 0
    blocks = []
    for kv, key_segs in zip(kv_sets, seg_sets):
        allowed = (query_segs[:, None] == key_segs[None, :]) & live
        key_heads = kv[:, :slot].reshape(kv.shape[0], slot_heads, HEAD)
        value_heads = kv[:, slot:].reshape(kv.shape[0], slot_heads, HEAD)
        scores = jnp.where(allowed[None], key_scores(query_heads, key_heads), masked_score)
        blocks.append((scores, allowed, value_heads))
    row_top = blocks[0][0].max(axis=2, keepdims=True)
    for scores, _, _ in blocks[1:]:
        row_top = jnp.maximum(row_top, scores.max(axis=2, keepdims=True))
    row_total = None
    mixed_out = None
    for scores, allowed, value_heads in blocks:
        exp_terms = jnp.where(allowed[None], jnp.exp(scores - row_top), 0.0)
        total = jnp.sum(exp_terms, axis=2)
        part = jnp.einsum(
            "hrk,khd->rhd", exp_terms.astype(jnp.bfloat16), value_heads,
            preferred_element_type=jnp.float32,
        )
        row_total = total if row_total is None else row_total + total
        mixed_out = part if mixed_out is None else mixed_out + part
    row_total = jnp.maximum(row_total, 1.0)
    mixed = (mixed_out / row_total.T[:, :, None]).reshape(chunk, slot).astype(jnp.bfloat16)

    mine = lax.dynamic_slice_in_dim(mixed, c * row_count, row_count)
    theirs = lax.dynamic_slice_in_dim(mixed, (1 - c) * row_count, row_count)
    back = cyclic(theirs, "core", 1)
    overlap = 2 * slot - width
    attended = jnp.where(
        first,
        jnp.concatenate([mine, back[:, overlap:]], axis=1),
        jnp.concatenate([back[:, : width - slot], mine], axis=1),
    )

    merged = attended.reshape(row_count // 4, 4 * width)
    piece = merged.shape[0]
    m_right = cyclic(merged, "x", -1)
    m_left = cyclic(merged, "x", 1)
    m_far = jnp.concatenate(
        [cyclic(m_right[: piece // 2], "x", -1), cyclic(m_left[piece // 2 :], "x", 1)], axis=0
    )
    gathered = jnp.zeros((piece * chips, merged.shape[1]), merged.dtype)
    for part, dx in zip((merged, m_right, m_left, m_far), (0, 1, chips - 1, 2)):
        at = (xi + dx) % chips
        gathered = lax.dynamic_update_slice_in_dim(gathered, part, at * piece, 0)
    projected = jnp.dot(gathered, chip_weight, preferred_element_type=jnp.float32)
    own_begin = b * block_len
    block_segs = lax.dynamic_slice_in_dim(segment_ids, own_begin, block_len)[::4]
    row_segs = lax.dynamic_index_in_dim(
        block_segs.reshape(chips, cores, piece), c, axis=1, keepdims=False
    ).reshape(chips * piece)
    member = row_segs[:, None] == jnp.arange(group_count, dtype=jnp.int32)[None, :]
    squares = jnp.sum(projected * projected, axis=1)
    seg_sums = jnp.sum(jnp.where(member, squares[:, None], 0.0), axis=0)
    row_peak = jnp.max(jnp.where(member, jnp.max(projected, axis=1)[:, None], masked_score), axis=0)
    all_segs = segment_ids[::4]
    all_member = all_segs[:, None] == jnp.arange(group_count, dtype=jnp.int32)[None, :]
    seg_counts = jnp.sum(all_member.astype(jnp.float32), axis=0) * (
        proj_weight.shape[1] * chips * cores
    )
    seg_sums, row_peak = butterfly(seg_sums, row_peak)
    seg_scale = lax.rsqrt(seg_sums / seg_counts + epsilon)
    row_scale = jnp.sum(jnp.where(member, seg_scale[None, :], 0.0), axis=1)
    normed_pair = (projected * row_scale[:, None]).astype(jnp.bfloat16)
    cols_out = proj_weight.shape[1]
    mine_out = lax.dynamic_slice_in_dim(normed_pair, c * cols_out, cols_out, axis=1)
    theirs_out = lax.dynamic_slice_in_dim(normed_pair, (1 - c) * cols_out, cols_out, axis=1)
    back_out = cyclic(theirs_out, "core", 1)
    mine_out = mine_out.reshape(chips, 1, piece, cols_out)
    back_out = back_out.reshape(chips, 1, piece, cols_out)
    normed = jnp.where(
        first,
        jnp.concatenate([mine_out, back_out], axis=1),
        jnp.concatenate([back_out, mine_out], axis=1),
    ).reshape(chips * cores * piece, cols_out)
    return (normed, row_peak * seg_scale)


def solution(mesh):
    blk, tp = mesh.devices.shape
    cores = 2
    chip_mesh = Mesh(mesh.devices.reshape(blk, tp // cores, cores), ALL)
    rows = P(ALL, None)
    in_specs = (rows, rows, rows, P(), P(None, ("x", "core")))
    out_specs = (P("blk", ("x", "core")), P())
    return jax.shard_map(
        per_device, mesh=chip_mesh, in_specs=in_specs, out_specs=out_specs, check_vma=False
    )
```

```python
import jax
import jax.numpy as jnp
from jax import lax
from jax.sharding import Mesh
from jax.sharding import PartitionSpec as P

HEAD = 128


masked_score = -1e30
epsilon = 1e-06

ALL = ("blk", "x", "core")


def key_scores(query_heads, key_heads):
    return jnp.einsum(
        "rhd,khd->hrk", query_heads, key_heads, preferred_element_type=jnp.float32
    ) * HEAD ** (-0.5)


def finish(scores, allowed, value_heads):
    scores = jnp.where(allowed[None], scores, masked_score)
    row_top = jnp.max(scores, axis=2, keepdims=True)
    exp_terms = jnp.where(allowed[None], jnp.exp(scores - row_top), 0.0)
    row_total = jnp.maximum(jnp.sum(exp_terms, axis=2), 1.0)
    weights = exp_terms.astype(jnp.bfloat16)
    mixed_out = jnp.einsum("hrk,khd->rhd", weights, value_heads, preferred_element_type=jnp.float32)
    return mixed_out / row_total.T[:, :, None]


def shifted(x, axis, by):
    n = lax.axis_size(axis)
    return lax.ppermute(x, axis, [(i, i + by) for i in range(n) if 0 <= i + by < n])


def cyclic(x, axis, by):
    n = lax.axis_size(axis)
    return lax.ppermute(x, axis, [(i, (i + by) % n) for i in range(n)])


def butterfly(sums, peaks):
    n = 1
    for name in ALL:
        n *= lax.axis_size(name)
    bit = 1
    while bit < n:
        perm = [(i, i ^ bit) for i in range(n)]
        other = lax.ppermute(jnp.stack([sums, peaks]), ALL, perm)
        sums = sums + other[0]
        peaks = jnp.maximum(peaks, other[1])
        bit *= 2
    return sums, peaks


def per_device(queries, keys, values, segment_ids, proj_weight):
    group_count = lax.axis_size("blk")
    chips = lax.axis_size("x")
    cores = lax.axis_size("core")
    b = lax.axis_index("blk")
    xi = lax.axis_index("x")
    c = lax.axis_index("core")
    row_count, width = queries.shape
    heads_count = width // HEAD
    slot_heads = -(-heads_count // cores)
    slot = slot_heads * HEAD
    block_len = segment_ids.shape[0] // group_count
    chunk = row_count * cores
    chip_begin = b * block_len + xi * chunk

    my_col = c * (width - slot)
    sib_col = (1 - c) * (width - slot)

    def cols(a, at):
        return lax.dynamic_slice_in_dim(a, at, slot, axis=1)

    own = jnp.concatenate([cols(keys, my_col), cols(values, my_col)], axis=1)
    give = jnp.concatenate([cols(keys, sib_col), cols(values, sib_col)], axis=1)
    got = cyclic(give, "core", 1)
    first = c == 0
    kv_chip = jnp.concatenate([jnp.where(first, own, got), jnp.where(first, got, own)], axis=0)
    own_q = cols(queries, my_col)
    got_q = cyclic(cols(queries, sib_col), "core", 1)
    q_chip = jnp.concatenate([jnp.where(first, own_q, got_q), jnp.where(first, got_q, own_q)], axis=0)

    right_a = cyclic(kv_chip[:row_count], "x", -1)
    left_b = cyclic(kv_chip[row_count:], "x", 1)
    right_a, left_b, rest = lax.optimization_barrier((right_a, left_b, kv_chip))
    right_b = cyclic(rest[row_count:], "x", -1)
    left_a = cyclic(rest[:row_count], "x", 1)
    from_right = jnp.concatenate([right_a, right_b], axis=0)
    from_left = jnp.concatenate([left_a, left_b], axis=0)
    relay = jnp.concatenate([cyclic(right_a, "x", -1), cyclic(left_b, "x", 1)], axis=0)
    kv_prev = shifted(kv_chip, "blk", 1)
    kv_next = shifted(kv_chip, "blk", -1)

    padded_segs = jnp.concatenate(
        [jnp.full((block_len,), -2, jnp.int32), segment_ids, jnp.full((block_len,), -2, jnp.int32)]
    )

    def segs_at(begin, length):
        return lax.dynamic_slice_in_dim(padded_segs, begin + block_len, length)

    kv_sets = [kv_chip, from_right, from_left, relay, kv_prev, kv_next]
    seg_sets = [
        segs_at(b * block_len + xi * chunk, chunk),
        segs_at(b * block_len + ((xi + 1) % chips) * chunk, chunk),
        segs_at(b * block_len + ((xi + chips - 1) % chips) * chunk, chunk),
        segs_at(b * block_len + ((xi + 2) % chips) * chunk, chunk),
        segs_at((b - 1) * block_len + xi * chunk, chunk),
        segs_at((b + 1) * block_len + xi * chunk, chunk),
    ]
    half = chips // 2
    far = relay
    pairs = []
    for bb in range(group_count):
        for xx in range(chips):
            for cc in range(cores):
                to = bb + 1 if xx < half else bb - 1
                if 0 <= to < group_count:
                    pairs.append(((bb * chips + xx) * cores + cc, (to * chips + xx) * cores + cc))
    kv_sets.append(lax.ppermute(far, ALL, pairs))
    seg_sets.append(
        segs_at(
            jnp.where(
                xi < half,
                (b - 1) * block_len + (xi + half) * chunk,
                (b + 1) * block_len + (xi - half) * chunk,
            ),
            chunk,
        )
    )
    for s in (1, chips - 1):
        send = jnp.where(xi >= s, kv_prev, kv_next)
        kv_sets.append(cyclic(send, "x", -s))
        src = xi + s
        begin = jnp.where(
            src < chips,
            (b - 1) * block_len + src * chunk,
            (b + 1) * block_len + (src - chips) * chunk,
        )
        seg_sets.append(segs_at(begin, chunk))

    query_segs = lax.dynamic_slice_in_dim(segment_ids, chip_begin, chunk)
    query_heads = q_chip.reshape(chunk, slot_heads, HEAD)
    live = query_segs[:, None] >= 0
    blocks = []
    for kv, key_segs in zip(kv_sets, seg_sets):
        allowed = (query_segs[:, None] == key_segs[None, :]) & live
        key_heads = kv[:, :slot].reshape(kv.shape[0], slot_heads, HEAD)
        value_heads = kv[:, slot:].reshape(kv.shape[0], slot_heads, HEAD)
        scores = jnp.where(allowed[None], key_scores(query_heads, key_heads), masked_score)
        blocks.append((scores, allowed, value_heads))
    row_top = blocks[0][0].max(axis=2, keepdims=True)
    for scores, _, _ in blocks[1:]:
        row_top = jnp.maximum(row_top, scores.max(axis=2, keepdims=True))
    row_total = None
    mixed_out = None
    for scores, allowed, value_heads in blocks:
        exp_terms = jnp.where(allowed[None], jnp.exp(scores - row_top), 0.0)
        total = jnp.sum(exp_terms, axis=2)
        part = jnp.einsum(
            "hrk,khd->rhd", exp_terms.astype(jnp.bfloat16), value_heads,
            preferred_element_type=jnp.float32,
        )
        row_total = total if row_total is None else row_total + total
        mixed_out = part if mixed_out is None else mixed_out + part
    row_total = jnp.maximum(row_total, 1.0)
    mixed = (mixed_out / row_total.T[:, :, None]).reshape(chunk, slot).astype(jnp.bfloat16)

    mine = lax.dynamic_slice_in_dim(mixed, c * row_count, row_count)
    theirs = lax.dynamic_slice_in_dim(mixed, (1 - c) * row_count, row_count)
    back = cyclic(theirs, "core", 1)
    overlap = 2 * slot - width
    attended = jnp.where(
        first,
        jnp.concatenate([mine, back[:, overlap:]], axis=1),
        jnp.concatenate([back[:, : width - slot], mine], axis=1),
    )

    merged = attended.reshape(row_count // 4, 4 * width)
    piece = merged.shape[0]
    m_right = cyclic(merged, "x", -1)
    m_left = cyclic(merged, "x", 1)
    m_far = jnp.concatenate(
        [cyclic(m_right[: piece // 2], "x", -1), cyclic(m_left[piece // 2 :], "x", 1)], axis=0
    )
    mine4 = jnp.stack([merged, m_right, m_left, m_far])
    sib4 = cyclic(mine4, "core", 1)
    gathered = jnp.zeros((piece * chips * cores, merged.shape[1]), merged.dtype)
    for k, dx in enumerate((0, 1, chips - 1, 2)):
        at = (xi + dx) % chips
        gathered = lax.dynamic_update_slice_in_dim(gathered, mine4[k], (at * cores + c) * piece, 0)
        gathered = lax.dynamic_update_slice_in_dim(gathered, sib4[k], (at * cores + 1 - c) * piece, 0)
    projected = jnp.dot(gathered, proj_weight, preferred_element_type=jnp.float32)
    own_begin = b * block_len
    row_segs = lax.dynamic_slice_in_dim(segment_ids, own_begin, block_len)[::4]
    member = row_segs[:, None] == jnp.arange(group_count, dtype=jnp.int32)[None, :]
    squares = jnp.sum(projected * projected, axis=1)
    seg_sums = jnp.sum(jnp.where(member, squares[:, None], 0.0), axis=0)
    row_peak = jnp.max(jnp.where(member, jnp.max(projected, axis=1)[:, None], masked_score), axis=0)
    all_segs = segment_ids[::4]
    all_member = all_segs[:, None] == jnp.arange(group_count, dtype=jnp.int32)[None, :]
    seg_counts = jnp.sum(all_member.astype(jnp.float32), axis=0) * (
        projected.shape[1] * chips * cores
    )
    seg_sums, row_peak = butterfly(seg_sums, row_peak)
    seg_scale = lax.rsqrt(seg_sums / seg_counts + epsilon)
    row_scale = jnp.sum(jnp.where(member, seg_scale[None, :], 0.0), axis=1)
    normed = (projected * row_scale[:, None]).astype(jnp.bfloat16)
    return (normed, row_peak * seg_scale)


def solution(mesh):
    blk, tp = mesh.devices.shape
    cores = 2
    chip_mesh = Mesh(mesh.devices.reshape(blk, tp // cores, cores), ALL)
    rows = P(ALL, None)
    in_specs = (rows, rows, rows, P(), P(None, ("x", "core")))
    out_specs = (P("blk", ("x", "core")), P())
    return jax.shard_map(
        per_device, mesh=chip_mesh, in_specs=in_specs, out_specs=out_specs, check_vma=False
    )
```

```python
import jax
import jax.numpy as jnp
from jax import lax
from jax.sharding import Mesh
from jax.sharding import PartitionSpec as P

HEAD = 128


masked_score = -1e30
epsilon = 1e-06

ALL = ("blk", "x", "core")


def key_scores(query_heads, key_heads):
    return jnp.einsum(
        "rhd,khd->hrk", query_heads, key_heads, preferred_element_type=jnp.float32
    ) * HEAD ** (-0.5)


def finish(scores, allowed, value_heads):
    scores = jnp.where(allowed[None], scores, masked_score)
    row_top = jnp.max(scores, axis=2, keepdims=True)
    exp_terms = jnp.where(allowed[None], jnp.exp(scores - row_top), 0.0)
    row_total = jnp.maximum(jnp.sum(exp_terms, axis=2), 1.0)
    weights = exp_terms.astype(jnp.bfloat16)
    mixed_out = jnp.einsum("hrk,khd->rhd", weights, value_heads, preferred_element_type=jnp.float32)
    return mixed_out / row_total.T[:, :, None]


def shifted(x, axis, by):
    n = lax.axis_size(axis)
    return lax.ppermute(x, axis, [(i, i + by) for i in range(n) if 0 <= i + by < n])


def cyclic(x, axis, by):
    n = lax.axis_size(axis)
    return lax.ppermute(x, axis, [(i, (i + by) % n) for i in range(n)])


def butterfly(sums, peaks):
    n = 1
    for name in ALL:
        n *= lax.axis_size(name)
    bit = n // 2
    while bit >= 1:
        perm = [(i, i ^ bit) for i in range(n)]
        other = lax.ppermute(jnp.stack([sums, peaks]), ALL, perm)
        sums = sums + other[0]
        peaks = jnp.maximum(peaks, other[1])
        bit //= 2
    return sums, peaks


def per_device(queries, keys, values, segment_ids, proj_weight):
    group_count = lax.axis_size("blk")
    chips = lax.axis_size("x")
    cores = lax.axis_size("core")
    b = lax.axis_index("blk")
    xi = lax.axis_index("x")
    c = lax.axis_index("core")
    row_count, width = queries.shape
    heads_count = width // HEAD
    slot_heads = -(-heads_count // cores)
    slot = slot_heads * HEAD
    block_len = segment_ids.shape[0] // group_count
    chunk = row_count * cores
    chip_begin = b * block_len + xi * chunk

    my_col = c * (width - slot)
    sib_col = (1 - c) * (width - slot)

    def cols(a, at):
        return lax.dynamic_slice_in_dim(a, at, slot, axis=1)

    own = jnp.concatenate([cols(keys, my_col), cols(values, my_col)], axis=1)
    give = jnp.concatenate([cols(keys, sib_col), cols(values, sib_col)], axis=1)
    got = cyclic(give, "core", 1)
    first = c == 0
    kv_chip = jnp.concatenate([jnp.where(first, own, got), jnp.where(first, got, own)], axis=0)
    own_q = cols(queries, my_col)
    got_q = cyclic(cols(queries, sib_col), "core", 1)
    q_chip = jnp.concatenate([jnp.where(first, own_q, got_q), jnp.where(first, got_q, own_q)], axis=0)

    right_a = cyclic(kv_chip[:row_count], "x", -1)
    left_b = cyclic(kv_chip[row_count:], "x", 1)
    right_a, left_b, rest = lax.optimization_barrier((right_a, left_b, kv_chip))
    right_b = cyclic(rest[row_count:], "x", -1)
    left_a = cyclic(rest[:row_count], "x", 1)
    from_right = jnp.concatenate([right_a, right_b], axis=0)
    from_left = jnp.concatenate([left_a, left_b], axis=0)
    relay = jnp.concatenate([cyclic(right_a, "x", -1), cyclic(left_b, "x", 1)], axis=0)
    kv_prev = shifted(kv_chip, "blk", 1)
    kv_next = shifted(kv_chip, "blk", -1)

    padded_segs = jnp.concatenate(
        [jnp.full((block_len,), -2, jnp.int32), segment_ids, jnp.full((block_len,), -2, jnp.int32)]
    )

    def segs_at(begin, length):
        return lax.dynamic_slice_in_dim(padded_segs, begin + block_len, length)

    kv_sets = [kv_chip, from_right, from_left, relay, kv_prev, kv_next]
    seg_sets = [
        segs_at(b * block_len + xi * chunk, chunk),
        segs_at(b * block_len + ((xi + 1) % chips) * chunk, chunk),
        segs_at(b * block_len + ((xi + chips - 1) % chips) * chunk, chunk),
        segs_at(b * block_len + ((xi + 2) % chips) * chunk, chunk),
        segs_at((b - 1) * block_len + xi * chunk, chunk),
        segs_at((b + 1) * block_len + xi * chunk, chunk),
    ]
    half = chips // 2
    far = relay
    pairs = []
    for bb in range(group_count):
        for xx in range(chips):
            for cc in range(cores):
                to = bb + 1 if xx < half else bb - 1
                if 0 <= to < group_count:
                    pairs.append(((bb * chips + xx) * cores + cc, (to * chips + xx) * cores + cc))
    kv_sets.append(lax.ppermute(far, ALL, pairs))
    seg_sets.append(
        segs_at(
            jnp.where(
                xi < half,
                (b - 1) * block_len + (xi + half) * chunk,
                (b + 1) * block_len + (xi - half) * chunk,
            ),
            chunk,
        )
    )
    for s in (1, chips - 1):
        send = jnp.where(xi >= s, kv_prev, kv_next)
        kv_sets.append(cyclic(send, "x", -s))
        src = xi + s
        begin = jnp.where(
            src < chips,
            (b - 1) * block_len + src * chunk,
            (b + 1) * block_len + (src - chips) * chunk,
        )
        seg_sets.append(segs_at(begin, chunk))

    query_segs = lax.dynamic_slice_in_dim(segment_ids, chip_begin, chunk)
    query_heads = q_chip.reshape(chunk, slot_heads, HEAD)
    live = query_segs[:, None] >= 0
    blocks = []
    for kv, key_segs in zip(kv_sets, seg_sets):
        allowed = (query_segs[:, None] == key_segs[None, :]) & live
        key_heads = kv[:, :slot].reshape(kv.shape[0], slot_heads, HEAD)
        value_heads = kv[:, slot:].reshape(kv.shape[0], slot_heads, HEAD)
        scores = jnp.where(allowed[None], key_scores(query_heads, key_heads), masked_score)
        blocks.append((scores, allowed, value_heads))
    row_top = blocks[0][0].max(axis=2, keepdims=True)
    for scores, _, _ in blocks[1:]:
        row_top = jnp.maximum(row_top, scores.max(axis=2, keepdims=True))
    row_total = None
    mixed_out = None
    for scores, allowed, value_heads in blocks:
        exp_terms = jnp.where(allowed[None], jnp.exp(scores - row_top), 0.0)
        total = jnp.sum(exp_terms, axis=2)
        part = jnp.einsum(
            "hrk,khd->rhd", exp_terms.astype(jnp.bfloat16), value_heads,
            preferred_element_type=jnp.float32,
        )
        row_total = total if row_total is None else row_total + total
        mixed_out = part if mixed_out is None else mixed_out + part
    row_total = jnp.maximum(row_total, 1.0)
    mixed = (mixed_out / row_total.T[:, :, None]).reshape(chunk, slot).astype(jnp.bfloat16)

    mine = lax.dynamic_slice_in_dim(mixed, c * row_count, row_count)
    theirs = lax.dynamic_slice_in_dim(mixed, (1 - c) * row_count, row_count)
    back = cyclic(theirs, "core", 1)
    overlap = 2 * slot - width
    attended = jnp.where(
        first,
        jnp.concatenate([mine, back[:, overlap:]], axis=1),
        jnp.concatenate([back[:, : width - slot], mine], axis=1),
    )

    merged = attended.reshape(row_count // 4, 4 * width)
    piece = merged.shape[0]
    m_right = cyclic(merged, "x", -1)
    m_left = cyclic(merged, "x", 1)
    m_far = jnp.concatenate(
        [cyclic(m_right[: piece // 2], "x", -1), cyclic(m_left[piece // 2 :], "x", 1)], axis=0
    )
    mine4 = jnp.stack([merged, m_right, m_left, m_far])
    sib4 = cyclic(mine4, "core", 1)
    gathered = jnp.zeros((piece * chips * cores, merged.shape[1]), merged.dtype)
    for k, dx in enumerate((0, 1, chips - 1, 2)):
        at = (xi + dx) % chips
        gathered = lax.dynamic_update_slice_in_dim(gathered, mine4[k], (at * cores + c) * piece, 0)
        gathered = lax.dynamic_update_slice_in_dim(gathered, sib4[k], (at * cores + 1 - c) * piece, 0)
    projected = jnp.dot(gathered, proj_weight, preferred_element_type=jnp.float32)
    own_begin = b * block_len
    row_segs = lax.dynamic_slice_in_dim(segment_ids, own_begin, block_len)[::4]
    member = row_segs[:, None] == jnp.arange(group_count, dtype=jnp.int32)[None, :]
    squares = jnp.sum(projected * projected, axis=1)
    seg_sums = jnp.sum(jnp.where(member, squares[:, None], 0.0), axis=0)
    row_peak = jnp.max(jnp.where(member, jnp.max(projected, axis=1)[:, None], masked_score), axis=0)
    all_segs = segment_ids[::4]
    all_member = all_segs[:, None] == jnp.arange(group_count, dtype=jnp.int32)[None, :]
    seg_counts = jnp.sum(all_member.astype(jnp.float32), axis=0) * (
        projected.shape[1] * chips * cores
    )
    seg_sums, row_peak = butterfly(seg_sums, row_peak)
    seg_scale = lax.rsqrt(seg_sums / seg_counts + epsilon)
    row_scale = jnp.sum(jnp.where(member, seg_scale[None, :], 0.0), axis=1)
    normed = (projected * row_scale[:, None]).astype(jnp.bfloat16)
    return (normed, row_peak * seg_scale)


def solution(mesh):
    blk, tp = mesh.devices.shape
    cores = 2
    chip_mesh = Mesh(mesh.devices.reshape(blk, tp // cores, cores), ALL)
    rows = P(ALL, None)
    in_specs = (rows, rows, rows, P(), P(None, ("x", "core")))
    out_specs = (P("blk", ("x", "core")), P())
    return jax.shard_map(
        per_device, mesh=chip_mesh, in_specs=in_specs, out_specs=out_specs, check_vma=False
    )
```
